128 devices in a mesh: expert: 32 (over y, z, core), dp: 4 (over x).
Axes of the slice: x: 4, y: 4, z: 4, core: 2. Of those that a mesh axis runs over, the one named last changes fastest.
Arguments:
- activations: bfloat16 [2048, 7168], P(('expert', 'dp')), may hold values from -6 to 6
- cotangent: bfloat16 [2048, 7168], P(('expert', 'dp')), may hold values from -6 to 6
- route_ids: int32 [2048, 8], P(('expert', 'dp')), may hold values from 0 to 31, all different within a row; in each aligned block of 16 rows (0 to 15, 16 to 31, ...) at most 5 rows name the same one
- route_weights: float32 [2048, 8], P(('expert', 'dp')), may hold values from 0.05 to 0.6
- gate_weights: bfloat16 [32, 7168, 1024], P('expert', 'dp'), may hold values from -0.0625 to 0.0625
- up_weights: bfloat16 [32, 7168, 1024], P('expert', 'dp'), may hold values from -0.0625 to 0.0625
- down_weights: bfloat16 [32, 1024, 7168], P('expert', None, 'dp'), may hold values from -0.1875 to 0.1875
Outputs:
- grad_input: bfloat16 [2048, 7168], P(('expert', 'dp'))
- grad_gate: bfloat16 [32, 7168, 1024], P('expert', 'dp')
- grad_up: bfloat16 [32, 7168, 1024], P('expert', 'dp')
- grad_down: bfloat16 [32, 1024, 7168], P('expert', None, 'dp')
The draws below stay inside these ranges and needn't reach their ends.
Inputs may be any that keep to these rules, and one draw needn't show every extreme that they name: `route_ids`: each token names 8 different experts. Among the routes of one device's 16 tokens, no expert is named more than 5 times, a bound that some block reaches.
All inputs are finite; a program needn't handle non-finite values.
Results may differ from the reference program's by a relative error of at most 0.0064.
Values may be sent and summed in bfloat16 or wider, within the bound.
No kernel may reach another device: no remote copies, remote signals or barrier semaphores. Data moves between devices by JAX's collectives and lax.ppermute only.
A program may use at most 128 MiB of HBM per device.

```python
import math
import jax
import jax.numpy as jnp
import numpy as np
from jax import lax

D = 7168
H = 1024
TOPK = 8
TOK_DEV = 16
EXPERTS = 32
CAP = 5
TOKENS = 2048


def steps_of(key, dims, shards, least, high):
    gain = 1.0
    for dim, parts in shards:
        steps = jax.random.uniform(jax.random.fold_in(jax.random.fold_in(key, 6), dim), (parts,), jnp.float32, least / len(shards), high / len(shards))
        gain = gain * jnp.repeat(jnp.exp(steps), dims[dim] // parts).reshape((-1,) + (1,) * (len(dims) - 1 - dim))
    return gain


def shared_out(rng, own, number, rows, count, top, limit, skew):
    order = jax.random.permutation(rng, count)
    crowded, ordinary = load_shares(count, rows * top, limit, skew, True), load_shares(count, rows * top, limit, skew, False)
    places = jnp.arange(count)

    def named(lengths, rotation):
        used = int((lengths > 0).sum())
        fixed = max(1, used // 4)
        passed = fixed + (places - fixed + rotation * (used - fixed)) % max(1, count - fixed)
        return jnp.zeros((count,), jnp.int32).at[order[jnp.where(places < fixed, places, passed)]].set(jnp.asarray(lengths, jnp.int32))

    lengths = jnp.where(number % 4 == 0, named(crowded, number // 4), named(ordinary, number - number // 4 - 1))
    mixed = jax.random.permutation(jax.random.fold_in(own, 3), count)
    donor, receiver = mixed[0:count // 2 * 2:2], mixed[1:count // 2 * 2:2]
    slack = jnp.minimum(lengths[donor] - 1, limit - lengths[receiver]) // 2
    slack = jnp.where((donor == order[0]) | (receiver == order[0]) | (lengths[receiver] == 0), 0, jnp.maximum(slack, 0))
    passed = jax.random.randint(jax.random.fold_in(own, 4), (count // 2,), 0, 1 << 20) % (slack + 1)
    lengths = lengths.at[donor].add(-passed).at[receiver].add(passed)
    members = jnp.searchsorted(jnp.cumsum(lengths), jnp.arange(rows * top), side="right").astype(jnp.int32)
    listing = members.reshape(top, rows).T
    listing = listing[jax.random.permutation(jax.random.fold_in(own, 1), rows)]
    rotation = jax.random.randint(jax.random.fold_in(own, 2), (rows, 1), 0, top)
    return jnp.take_along_axis(listing, (jnp.arange(top)[None, :] + rotation) % top, axis=1)


def load_shares(count, total, limit, slope, full):
    weights = [(1 << 20) // math.isqrt(rank ** slope) + 1 for rank in range(1, count + 1)]
    largest = limit if full else min(limit, max(-(-total // count), total * weights[0] // sum(weights)))
    least = 1 if total - largest >= count - 1 else 0
    counts, surplus = [largest] + [least] * (count - 1), total - largest - least * (count - 1)
    while surplus > 0:
        movable = [i for i in range(1, count) if counts[i] < largest] or [i for i in range(1, count) if counts[i] < limit]
        pool, remaining = sum([weights[i] for i in movable]), surplus
        for i in movable:
            addition = min(limit - counts[i], max(1, remaining * weights[i] // pool), surplus)
            counts[i] = counts[i] + addition
            surplus = surplus - addition
    return np.array(counts)


def normal_values(stream_key, extent, width, limit, cuts=(), held_as=jnp.bfloat16):
    values = jax.random.normal(stream_key, extent, jnp.float32) * width
    if len(cuts) > 0:
        values = steps_of(stream_key, extent, cuts, -0.22, 0.18) * values
    return jnp.clip(values, min=-limit, max=limit).astype(held_as)


def setup_inputs(seed: int = 0) -> dict:
    streams_of = jax.random.split(jax.random.key(seed), 8)
    activations = normal_values(streams_of[0], (TOKENS, D), 1.0, 6.0, ((0, 128),))
    cotangent = normal_values(streams_of[1], (TOKENS, D), 1.0, 6.0, ((0, 128),))
    route_ids_keys = jax.random.split(jax.random.fold_in(streams_of[2], 1), TOKENS // TOK_DEV)
    route_ids_turns = jax.random.permutation(jax.random.fold_in(streams_of[2], 3), TOKENS // TOK_DEV)
    route_ids = jax.vmap(lambda own, number: shared_out(jax.random.fold_in(streams_of[2], 2), own, number, TOK_DEV, EXPERTS, TOPK, CAP, 2))(route_ids_keys, route_ids_turns).reshape((TOKENS, TOPK))
    route_weights = jnp.clip(0.05 + 0.55 * jax.random.uniform(streams_of[3], (TOKENS, TOPK), jnp.float32) ** steps_of(streams_of[3], (TOKENS, TOPK), ((0, 128),), -0.2, 0.2), 0.05, 0.6)
    gate_weights = normal_values(streams_of[4], (EXPERTS, D, H), D ** -0.5, 0.0625, ((0, 32), (1, 4)))
    up_weights = normal_values(streams_of[5], (EXPERTS, D, H), D ** -0.5, 0.0625, ((0, 32), (1, 4)))
    down_weights = normal_values(streams_of[6], (EXPERTS, H, D), H ** -0.5, 0.1875, ((0, 32), (2, 4)))
    return {"activations": activations, "cotangent": cotangent, "route_ids": route_ids, "route_weights": route_weights, "gate_weights": gate_weights, "up_weights": up_weights, "down_weights": down_weights}


def swiglu_back(gate, upper, upstream):
    sigma = jax.nn.sigmoid(gate)
    silu_gate = gate * sigma
    activated = (silu_gate * upper).astype(jnp.bfloat16)
    grad_pre = (upstream * upper * sigma * (1.0 + gate * (1.0 - sigma))).astype(jnp.bfloat16)
    grad_lin = (upstream * silu_gate).astype(jnp.bfloat16)
    return grad_pre, grad_lin, activated


def reference(activations, cotangent, route_ids, route_weights, gate_weights, up_weights, down_weights):
    tokens = activations.shape[0]
    blocks = tokens // TOK_DEV
    block_ids = route_ids.reshape(blocks, TOK_DEV * TOPK)
    onehot = (block_ids[:, :, None] == jnp.arange(EXPERTS, dtype=jnp.int32)[None, None, :]).astype(jnp.int32)
    before = jnp.cumsum(onehot, axis=1) - onehot
    slot = jnp.sum(before * onehot, axis=2).astype(jnp.int32)
    row_index = (jnp.arange(blocks, dtype=jnp.int32)[:, None] * CAP + slot).reshape(-1).astype(jnp.int32)
    flat_ids = route_ids.reshape(-1).astype(jnp.int32)
    token_of = (jnp.arange(tokens * TOPK, dtype=jnp.int32) // TOPK).astype(jnp.int32)
    source = jnp.full((EXPERTS, blocks * CAP), tokens, jnp.int32).at[flat_ids, row_index].set(token_of)
    weight = jnp.zeros((EXPERTS, blocks * CAP), jnp.float32).at[flat_ids, row_index].set(route_weights.reshape(-1))
    act_pad = jnp.concatenate([activations, jnp.zeros((1, D), activations.dtype)], axis=0)
    cot_pad = jnp.concatenate([cotangent, jnp.zeros((1, D), cotangent.dtype)], axis=0)

    def one_expert(grad_rows, inputs):
        src, wgt, gate_w, up_w, down_w = inputs
        expert_input = act_pad[src]
        expert_cot = (cot_pad[src].astype(jnp.float32) * wgt[:, None]).astype(jnp.bfloat16)
        gate = jnp.dot(expert_input, gate_w, preferred_element_type=jnp.float32)
        upper = jnp.dot(expert_input, up_w, preferred_element_type=jnp.float32)
        upstream = jnp.dot(expert_cot, down_w.T, preferred_element_type=jnp.float32)
        grad_pre, grad_lin, activated = swiglu_back(gate, upper, upstream)
        g_gate = jnp.dot(expert_input.T, grad_pre, preferred_element_type=jnp.float32).astype(jnp.bfloat16)
        g_up = jnp.dot(expert_input.T, grad_lin, preferred_element_type=jnp.float32).astype(jnp.bfloat16)
        g_down = jnp.dot(activated.T, expert_cot, preferred_element_type=jnp.float32).astype(jnp.bfloat16)
        contribution = (jnp.dot(grad_pre, gate_w.T, preferred_element_type=jnp.float32)
                        + jnp.dot(grad_lin, up_w.T, preferred_element_type=jnp.float32)).astype(jnp.bfloat16)
        grad_rows = grad_rows.at[src].add(contribution.astype(jnp.float32))
        return grad_rows, (g_gate, g_up, g_down)

    start_rows = jnp.zeros((tokens + 1, D), jnp.float32)
    grad_rows, grads = lax.scan(one_expert, start_rows, (source, weight, gate_weights, up_weights, down_weights))
    grad_input = grad_rows[:tokens].astype(jnp.bfloat16)
    return grad_input, grads[0], grads[1], grads[2]
```

```python
import jax
import jax.numpy as jnp
from jax import lax
from jax.sharding import PartitionSpec as P


def swiglu_back(gate, upper, upstream):
    sigma = jax.nn.sigmoid(gate)
    silu_gate = gate * sigma
    activated = (silu_gate * upper).astype(jnp.bfloat16)
    grad_pre = (upstream * upper * sigma * (1.0 + gate * (1.0 - sigma))).astype(jnp.bfloat16)
    grad_lin = (upstream * silu_gate).astype(jnp.bfloat16)
    return (grad_pre, grad_lin, activated)


def contract_rows(left, right):
    return lax.dot_general(
        left, right, (((0,), (0,)), ((), ())), preferred_element_type=jnp.float32
    )


def shards(
    activations, cotangent, route_ids, route_weights, gate_weights, up_weights, down_weights
):
    tok_rows, width = activations.shape
    topk = route_ids.shape[1]
    num_dp = lax.axis_size("dp")
    num_exp = lax.axis_size("expert")
    slice_width = gate_weights.shape[1]
    hidden = gate_weights.shape[2]
    capacity = min(tok_rows, 5 * tok_rows * topk // (4 * num_exp))
    buffer_rows = num_exp * num_dp * capacity
    flat_ids = route_ids.reshape(-1)
    expert_iota = jnp.arange(num_exp, dtype=jnp.int32)
    onehot = (flat_ids[:, None] == expert_iota[None, :]).astype(jnp.int32)
    before = jnp.cumsum(onehot, axis=0) - onehot
    slot = jnp.sum(before * onehot, axis=1)
    target = (flat_ids * capacity + slot).reshape(tok_rows, topk)
    slot_iota = jnp.arange(num_exp * capacity, dtype=jnp.int32)
    matches = target[:, :, None] == slot_iota[None, None, :]
    placing = jnp.any(matches, axis=1).astype(jnp.bfloat16)
    slot_weight = jnp.sum(jnp.where(matches, route_weights[:, :, None], 0.0), axis=(0, 1))
    send_act = contract_rows(placing, activations).astype(jnp.bfloat16)
    send_cot = (contract_rows(placing, cotangent) * slot_weight[:, None]).astype(jnp.bfloat16)
    send_act = send_act.reshape(num_exp, capacity, num_dp, slice_width)
    send_cot = send_cot.reshape(num_exp, capacity, num_dp, slice_width)
    send_both = jnp.concatenate([send_act, send_cot], axis=3)
    flat_both = jnp.swapaxes(send_both, 1, 2).reshape(
        num_exp * num_dp, capacity, 2 * slice_width
    )
    recv_both = lax.all_to_all(flat_both, ("expert", "dp"), split_axis=0, concat_axis=0, tiled=True)
    recv_both = recv_both.reshape(buffer_rows, 2 * slice_width)
    act_rows = recv_both[:, :slice_width]
    cot_rows = recv_both[:, slice_width:]
    gate_local = gate_weights[0]
    up_local = up_weights[0]
    down_local = down_weights[0]
    gate_part = jnp.dot(act_rows, gate_local, preferred_element_type=jnp.float32)
    up_part = jnp.dot(act_rows, up_local, preferred_element_type=jnp.float32)
    back_part = lax.dot_general(
        cot_rows, down_local, (((1,), (1,)), ((), ())), preferred_element_type=jnp.float32
    )
    summed = lax.psum_scatter(
        jnp.concatenate([gate_part, up_part, back_part], axis=1),
        "dp",
        scatter_dimension=0,
        tiled=True,
    )
    grad_pre, grad_lin, activated = swiglu_back(
        summed[:, :hidden], summed[:, hidden : 2 * hidden], summed[:, 2 * hidden :]
    )
    gathered = lax.all_gather(
        jnp.concatenate([grad_pre, grad_lin, activated], axis=1), "dp", axis=0, tiled=True
    )
    grad_pre = gathered[:, :hidden]
    grad_lin = gathered[:, hidden : 2 * hidden]
    activated = gathered[:, 2 * hidden :]
    rows_back = lax.dot_general(
        grad_pre, gate_local, (((1,), (1,)), ((), ())), preferred_element_type=jnp.float32
    ) + lax.dot_general(
        grad_lin, up_local, (((1,), (1,)), ((), ())), preferred_element_type=jnp.float32
    )
    grad_gate = contract_rows(act_rows, grad_pre).astype(jnp.bfloat16)[None]
    grad_up = contract_rows(act_rows, grad_lin).astype(jnp.bfloat16)[None]
    grad_down = contract_rows(activated, cot_rows).astype(jnp.bfloat16)[None]
    back_rows = rows_back.astype(jnp.bfloat16)
    flat_back = back_rows.reshape(num_exp * num_dp, capacity, slice_width)
    arrived = lax.all_to_all(flat_back, ("expert", "dp"), split_axis=0, concat_axis=0, tiled=True)
    arrived = jnp.swapaxes(arrived.reshape(num_exp, num_dp, capacity, slice_width), 1, 2)
    arrived = arrived.reshape(num_exp * capacity, width)
    grad_input = jnp.dot(placing, arrived, preferred_element_type=jnp.float32).astype(jnp.bfloat16)
    return (grad_input, grad_gate, grad_up, grad_down)


def solution(mesh):
    placed = (
        P(("expert", "dp"), None),
        P(("expert", "dp"), None),
        P(("expert", "dp"), None),
        P(("expert", "dp"), None),
        P("expert", "dp", None),
        P("expert", "dp", None),
        P("expert", None, "dp"),
    )
    return jax.shard_map(
        shards,
        mesh=mesh,
        in_specs=placed,
        out_specs=(
            P(("expert", "dp"), None),
            P("expert", "dp", None),
            P("expert", "dp", None),
            P("expert", None, "dp"),
        ),
        check_vma=False,
    )
```

```python
import jax
import jax.numpy as jnp
from jax import lax
from jax.sharding import PartitionSpec as P


def swiglu_back(gate, upper, upstream):
    sigma = jax.nn.sigmoid(gate)
    silu_gate = gate * sigma
    activated = (silu_gate * upper).astype(jnp.bfloat16)
    grad_pre = (upstream * upper * sigma * (1.0 + gate * (1.0 - sigma))).astype(jnp.bfloat16)
    grad_lin = (upstream * silu_gate).astype(jnp.bfloat16)
    return (grad_pre, grad_lin, activated)


def contract_rows(left, right):
    return lax.dot_general(
        left, right, (((0,), (0,)), ((), ())), preferred_element_type=jnp.float32
    )


def shards(
    activations, cotangent, route_ids, route_weights, gate_weights, up_weights, down_weights
):
    tok_rows, width = activations.shape
    topk = route_ids.shape[1]
    num_dp = lax.axis_size("dp")
    num_exp = lax.axis_size("expert")
    slice_width = gate_weights.shape[1]
    hidden = gate_weights.shape[2]
    capacity = min(tok_rows, 5 * tok_rows * topk // (4 * num_exp))
    buffer_rows = num_exp * num_dp * capacity
    flat_ids = route_ids.reshape(-1)
    expert_iota = jnp.arange(num_exp, dtype=jnp.int32)
    onehot = (flat_ids[:, None] == expert_iota[None, :]).astype(jnp.int32)
    before = jnp.cumsum(onehot, axis=0) - onehot
    slot = jnp.sum(before * onehot, axis=1)
    target = (flat_ids * capacity + slot).reshape(tok_rows, topk)
    slot_iota = jnp.arange(num_exp * capacity, dtype=jnp.int32)
    matches = target[:, :, None] == slot_iota[None, None, :]
    placing = jnp.any(matches, axis=1).astype(jnp.bfloat16)
    slot_weight = jnp.sum(jnp.where(matches, route_weights[:, :, None], 0.0), axis=(0, 1))
    send_act = contract_rows(placing, activations).astype(jnp.bfloat16)
    send_cot = (contract_rows(placing, cotangent) * slot_weight[:, None]).astype(jnp.bfloat16)
    send_act = send_act.reshape(num_exp, capacity, num_dp, slice_width)
    send_cot = send_cot.reshape(num_exp, capacity, num_dp, slice_width)
    send_both = jnp.concatenate([send_act, send_cot], axis=3)
    flat_both = jnp.swapaxes(send_both, 1, 2).reshape(
        num_exp * num_dp, capacity, 2 * slice_width
    )
    recv_both = lax.all_to_all(flat_both, ("expert", "dp"), split_axis=0, concat_axis=0, tiled=True)
    recv_both = recv_both.reshape(buffer_rows, 2 * slice_width)
    act_rows = recv_both[:, :slice_width]
    cot_rows = recv_both[:, slice_width:]
    gate_local = gate_weights[0]
    up_local = up_weights[0]
    down_local = down_weights[0]
    gate_part = jnp.dot(act_rows, gate_local, preferred_element_type=jnp.float32)
    up_part = jnp.dot(act_rows, up_local, preferred_element_type=jnp.float32)
    back_part = lax.dot_general(
        cot_rows, down_local, (((1,), (1,)), ((), ())), preferred_element_type=jnp.float32
    )
    parts = jnp.concatenate([gate_part, up_part, back_part], axis=1)
    quarter = buffer_rows // num_dp
    parts = parts.reshape(num_dp, quarter, 3 * hidden)
    me = lax.axis_index("dp")
    own = lax.dynamic_index_in_dim(parts, me, 0, keepdims=False)
    came = lax.all_to_all(
        parts.astype(jnp.bfloat16), "dp", split_axis=0, concat_axis=0, tiled=True
    )
    others = (jnp.arange(num_dp, dtype=jnp.int32) != me).astype(jnp.float32)
    summed = own + jnp.sum(came.astype(jnp.float32) * others[:, None, None], axis=0)
    grad_pre, grad_lin, activated = swiglu_back(
        summed[:, :hidden], summed[:, hidden : 2 * hidden], summed[:, 2 * hidden :]
    )
    gathered = lax.all_gather(
        jnp.concatenate([grad_pre, grad_lin, activated], axis=1), "dp", axis=0, tiled=True
    )
    grad_pre = gathered[:, :hidden]
    grad_lin = gathered[:, hidden : 2 * hidden]
    activated = gathered[:, 2 * hidden :]
    rows_back = lax.dot_general(
        grad_pre, gate_local, (((1,), (1,)), ((), ())), preferred_element_type=jnp.float32
    ) + lax.dot_general(
        grad_lin, up_local, (((1,), (1,)), ((), ())), preferred_element_type=jnp.float32
    )
    grad_gate = contract_rows(act_rows, grad_pre).astype(jnp.bfloat16)[None]
    grad_up = contract_rows(act_rows, grad_lin).astype(jnp.bfloat16)[None]
    grad_down = contract_rows(activated, cot_rows).astype(jnp.bfloat16)[None]
    back_rows = rows_back.astype(jnp.bfloat16)
    flat_back = back_rows.reshape(num_exp * num_dp, capacity, slice_width)
    arrived = lax.all_to_all(flat_back, ("expert", "dp"), split_axis=0, concat_axis=0, tiled=True)
    arrived = jnp.swapaxes(arrived.reshape(num_exp, num_dp, capacity, slice_width), 1, 2)
    arrived = arrived.reshape(num_exp * capacity, width)
    grad_input = jnp.dot(placing, arrived, preferred_element_type=jnp.float32).astype(jnp.bfloat16)
    return (grad_input, grad_gate, grad_up, grad_down)


def solution(mesh):
    placed = (
        P(("expert", "dp"), None),
        P(("expert", "dp"), None),
        P(("expert", "dp"), None),
        P(("expert", "dp"), None),
        P("expert", "dp", None),
        P("expert", "dp", None),
        P("expert", None, "dp"),
    )
    return jax.shard_map(
        shards,
        mesh=mesh,
        in_specs=placed,
        out_specs=(
            P(("expert", "dp"), None),
            P("expert", "dp", None),
            P("expert", "dp", None),
            P("expert", None, "dp"),
        ),
        check_vma=False,
    )
```

```python
import jax
import jax.numpy as jnp
from jax import lax
from jax.sharding import PartitionSpec as P


def swiglu_back(gate, upper, upstream):
    sigma = jax.nn.sigmoid(gate)
    silu_gate = gate * sigma
    activated = (silu_gate * upper).astype(jnp.bfloat16)
    grad_pre = (upstream * upper * sigma * (1.0 + gate * (1.0 - sigma))).astype(jnp.bfloat16)
    grad_lin = (upstream * silu_gate).astype(jnp.bfloat16)
    return (grad_pre, grad_lin, activated)


def contract_rows(left, right):
    return lax.dot_general(
        left, right, (((0,), (0,)), ((), ())), preferred_element_type=jnp.float32
    )


def exchange(parts, num_dp):
    rows, cols = parts.shape
    parts = parts.reshape(num_dp, rows // num_dp, cols)
    me = lax.axis_index("dp")
    own = lax.dynamic_index_in_dim(parts, me, 0, keepdims=False)
    came = lax.all_to_all(
        parts.astype(jnp.bfloat16), "dp", split_axis=0, concat_axis=0, tiled=True
    )
    others = (jnp.arange(num_dp, dtype=jnp.int32) != me).astype(jnp.float32)
    return own + jnp.sum(came.astype(jnp.float32) * others[:, None, None], axis=0)


def shards(
    activations, cotangent, route_ids, route_weights, gate_weights, up_weights, down_weights
):
    tok_rows, width = activations.shape
    topk = route_ids.shape[1]
    num_dp = lax.axis_size("dp")
    num_exp = lax.axis_size("expert")
    slice_width = gate_weights.shape[1]
    hidden = gate_weights.shape[2]
    capacity = min(tok_rows, 5 * tok_rows * topk // (4 * num_exp))
    flat_ids = route_ids.reshape(-1)
    expert_iota = jnp.arange(num_exp, dtype=jnp.int32)
    onehot = (flat_ids[:, None] == expert_iota[None, :]).astype(jnp.int32)
    before = jnp.cumsum(onehot, axis=0) - onehot
    slot = jnp.sum(before * onehot, axis=1)
    target = (flat_ids * capacity + slot).reshape(tok_rows, topk)
    slot_iota = jnp.arange(num_exp * capacity, dtype=jnp.int32)
    matches = target[:, :, None] == slot_iota[None, None, :]
    placing = jnp.any(matches, axis=1).astype(jnp.bfloat16)
    slot_weight = jnp.sum(jnp.where(matches, route_weights[:, :, None], 0.0), axis=(0, 1))
    send_act = contract_rows(placing, activations).astype(jnp.bfloat16)
    send_cot = (contract_rows(placing, cotangent) * slot_weight[:, None]).astype(jnp.bfloat16)
    send_act = send_act.reshape(num_exp, capacity, num_dp, slice_width)
    send_cot = send_cot.reshape(num_exp, capacity, num_dp, slice_width)
    send_both = jnp.swapaxes(jnp.concatenate([send_act, send_cot], axis=3), 1, 2)
    gate_local = gate_weights[0]
    up_local = up_weights[0]
    down_local = down_weights[0]
    split = (capacity + 1) // 2
    bounds = [(0, split), (split, capacity)]
    sums = [None, None, None]
    pieces = []
    for lo, hi in bounds:
        take = hi - lo
        flat_both = send_both[:, :, lo:hi].reshape(num_exp * num_dp, take, 2 * slice_width)
        recv_both = lax.all_to_all(
            flat_both, ("expert", "dp"), split_axis=0, concat_axis=0, tiled=True
        )
        recv_both = recv_both.reshape(num_exp * num_dp * take, 2 * slice_width)
        act_rows = recv_both[:, :slice_width]
        cot_rows = recv_both[:, slice_width:]
        gate_part = jnp.dot(act_rows, gate_local, preferred_element_type=jnp.float32)
        up_part = jnp.dot(act_rows, up_local, preferred_element_type=jnp.float32)
        back_part = lax.dot_general(
            cot_rows, down_local, (((1,), (1,)), ((), ())), preferred_element_type=jnp.float32
        )
        summed = exchange(jnp.concatenate([gate_part, up_part, back_part], axis=1), num_dp)
        grad_pre, grad_lin, activated = swiglu_back(
            summed[:, :hidden], summed[:, hidden : 2 * hidden], summed[:, 2 * hidden :]
        )
        gathered = lax.all_gather(
            jnp.concatenate([grad_pre, grad_lin, activated], axis=1), "dp", axis=0, tiled=True
        )
        grad_pre = gathered[:, :hidden]
        grad_lin = gathered[:, hidden : 2 * hidden]
        activated = gathered[:, 2 * hidden :]
        rows_back = lax.dot_general(
            grad_pre, gate_local, (((1,), (1,)), ((), ())), preferred_element_type=jnp.float32
        ) + lax.dot_general(
            grad_lin, up_local, (((1,), (1,)), ((), ())), preferred_element_type=jnp.float32
        )
        terms = (
            contract_rows(act_rows, grad_pre),
            contract_rows(act_rows, grad_lin),
            contract_rows(activated, cot_rows),
        )
        sums = [t if s is None else s + t for s, t in zip(sums, terms)]
        flat_back = rows_back.astype(jnp.bfloat16).reshape(num_exp * num_dp, take, slice_width)
        arrived = lax.all_to_all(
            flat_back, ("expert", "dp"), split_axis=0, concat_axis=0, tiled=True
        )
        pieces.append(arrived.reshape(num_exp, num_dp, take, slice_width))
    grad_gate, grad_up, grad_down = (s.astype(jnp.bfloat16)[None] for s in sums)
    arrived = jnp.swapaxes(jnp.concatenate(pieces, axis=2), 1, 2)
    arrived = arrived.reshape(num_exp * capacity, width)
    grad_input = jnp.dot(placing, arrived, preferred_element_type=jnp.float32).astype(jnp.bfloat16)
    return (grad_input, grad_gate, grad_up, grad_down)


def solution(mesh):
    placed = (
        P(("expert", "dp"), None),
        P(("expert", "dp"), None),
        P(("expert", "dp"), None),
        P(("expert", "dp"), None),
        P("expert", "dp", None),
        P("expert", "dp", None),
        P("expert", None, "dp"),
    )
    return jax.shard_map(
        shards,
        mesh=mesh,
        in_specs=placed,
        out_specs=(
            P(("expert", "dp"), None),
            P("expert", "dp", None),
            P("expert", "dp", None),
            P("expert", None, "dp"),
        ),
        check_vma=False,
    )
```

```python
import jax
import jax.numpy as jnp
from jax import lax
from jax.sharding import PartitionSpec as P


def swiglu_back(gate, upper, upstream):
    sigma = jax.nn.sigmoid(gate)
    silu_gate = gate * sigma
    activated = (silu_gate * upper).astype(jnp.bfloat16)
    grad_pre = (upstream * upper * sigma * (1.0 + gate * (1.0 - sigma))).astype(jnp.bfloat16)
    grad_lin = (upstream * silu_gate).astype(jnp.bfloat16)
    return (grad_pre, grad_lin, activated)


def contract_rows(left, right):
    return lax.dot_general(
        left, right, (((0,), (0,)), ((), ())), preferred_element_type=jnp.float32
    )


def exchange(parts, num_dp):
    rows, cols = parts.shape
    parts = parts.reshape(num_dp, rows // num_dp, cols)
    me = lax.axis_index("dp")
    own = lax.dynamic_index_in_dim(parts, me, 0, keepdims=False)
    came = lax.all_to_all(
        parts.astype(jnp.bfloat16), "dp", split_axis=0, concat_axis=0, tiled=True
    )
    others = (jnp.arange(num_dp, dtype=jnp.int32) != me).astype(jnp.float32)
    return own + jnp.sum(came.astype(jnp.float32) * others[:, None, None], axis=0)


def shards(
    activations, cotangent, route_ids, route_weights, gate_weights, up_weights, down_weights
):
    tok_rows, width = activations.shape
    topk = route_ids.shape[1]
    num_dp = lax.axis_size("dp")
    num_exp = lax.axis_size("expert")
    slice_width = gate_weights.shape[1]
    hidden = gate_weights.shape[2]
    capacity = min(tok_rows, 5 * tok_rows * topk // (4 * num_exp))
    flat_ids = route_ids.reshape(-1)
    expert_iota = jnp.arange(num_exp, dtype=jnp.int32)
    onehot = (flat_ids[:, None] == expert_iota[None, :]).astype(jnp.int32)
    before = jnp.cumsum(onehot, axis=0) - onehot
    slot = jnp.sum(before * onehot, axis=1)
    target = (flat_ids * capacity + slot).reshape(tok_rows, topk)
    slot_iota = jnp.arange(num_exp * capacity, dtype=jnp.int32)
    matches = target[:, :, None] == slot_iota[None, None, :]
    placing = jnp.any(matches, axis=1).astype(jnp.bfloat16)
    slot_weight = jnp.sum(jnp.where(matches, route_weights[:, :, None], 0.0), axis=(0, 1))
    by_slice = lambda a: jnp.swapaxes(a.reshape(tok_rows, num_dp, slice_width), 0, 1)
    both = jnp.concatenate([by_slice(activations), by_slice(cotangent)], axis=2)
    slots = placing.T.reshape(num_exp, capacity, tok_rows)
    scale = slot_weight.reshape(num_exp, capacity)
    gate_local = gate_weights[0]
    up_local = up_weights[0]
    down_local = down_weights[0]
    axes = ("dp", "expert")
    split = (capacity + 1) // 2
    bounds = [(0, split), (split, capacity)]
    sums = [None, None, None]
    pieces = []
    for lo, hi in bounds:
        take = hi - lo
        rows = num_exp * take
        pick = jnp.broadcast_to(slots[:, lo:hi].reshape(1, rows, tok_rows), (num_dp, rows, tok_rows))
        gathered_rows = lax.dot_general(
            pick, both, (((2,), (1,)), ((0,), (0,))), preferred_element_type=jnp.float32
        )
        weight = jnp.concatenate(
            [
                jnp.ones((rows, slice_width), jnp.float32),
                jnp.broadcast_to(scale[:, lo:hi].reshape(rows, 1), (rows, slice_width)),
            ],
            axis=1,
        )
        flat_both = (gathered_rows * weight[None]).astype(jnp.bfloat16)
        flat_both = flat_both.reshape(num_dp * num_exp, take, 2 * slice_width)
        recv_both = lax.all_to_all(flat_both, axes, split_axis=0, concat_axis=0, tiled=True)
        recv_both = recv_both.reshape(num_exp * num_dp * take, 2 * slice_width)
        act_rows = recv_both[:, :slice_width]
        cot_rows = recv_both[:, slice_width:]
        gate_part = jnp.dot(act_rows, gate_local, preferred_element_type=jnp.float32)
        up_part = jnp.dot(act_rows, up_local, preferred_element_type=jnp.float32)
        back_part = lax.dot_general(
            cot_rows, down_local, (((1,), (1,)), ((), ())), preferred_element_type=jnp.float32
        )
        summed = exchange(jnp.concatenate([gate_part, up_part, back_part], axis=1), num_dp)
        grad_pre, grad_lin, activated = swiglu_back(
            summed[:, :hidden], summed[:, hidden : 2 * hidden], summed[:, 2 * hidden :]
        )
        gathered = lax.all_gather(
            jnp.concatenate([grad_pre, grad_lin, activated], axis=1), "dp", axis=0, tiled=True
        )
        grad_pre = gathered[:, :hidden]
        grad_lin = gathered[:, hidden : 2 * hidden]
        activated = gathered[:, 2 * hidden :]
        rows_back = lax.dot_general(
            grad_pre, gate_local, (((1,), (1,)), ((), ())), preferred_element_type=jnp.float32
        ) + lax.dot_general(
            grad_lin, up_local, (((1,), (1,)), ((), ())), preferred_element_type=jnp.float32
        )
        terms = (
            contract_rows(act_rows, grad_pre),
            contract_rows(act_rows, grad_lin),
            contract_rows(activated, cot_rows),
        )
        sums = [t if s is None else s + t for s, t in zip(sums, terms)]
        flat_back = rows_back.astype(jnp.bfloat16).reshape(num_dp * num_exp, take, slice_width)
        arrived = lax.all_to_all(flat_back, axes, split_axis=0, concat_axis=0, tiled=True)
        pieces.append(arrived.reshape(num_dp, num_exp, take, slice_width))
    grad_gate, grad_up, grad_down = (s.astype(jnp.bfloat16)[None] for s in sums)
    arrived = jnp.concatenate(pieces, axis=2).reshape(num_dp, num_exp * capacity, slice_width)
    spread = jnp.broadcast_to(placing[None], (num_dp,) + placing.shape)
    grad_slices = lax.dot_general(
        spread, arrived, (((2,), (1,)), ((0,), (0,))), preferred_element_type=jnp.float32
    ).astype(jnp.bfloat16)
    grad_input = jnp.swapaxes(grad_slices, 0, 1).reshape(tok_rows, width)
    return (grad_input, grad_gate, grad_up, grad_down)


def solution(mesh):
    placed = (
        P(("expert", "dp"), None),
        P(("expert", "dp"), None),
        P(("expert", "dp"), None),
        P(("expert", "dp"), None),
        P("expert", "dp", None),
        P("expert", "dp", None),
        P("expert", None, "dp"),
    )
    return jax.shard_map(
        shards,
        mesh=mesh,
        in_specs=placed,
        out_specs=(
            P(("expert", "dp"), None),
            P("expert", "dp", None),
            P("expert", "dp", None),
            P("expert", None, "dp"),
        ),
        check_vma=False,
    )
```

```python
import jax
import jax.numpy as jnp
from jax import lax
from jax.sharding import PartitionSpec as P


def swiglu_back(gate, upper, upstream):
    sigma = jax.nn.sigmoid(gate)
    silu_gate = gate * sigma
    activated = (silu_gate * upper).astype(jnp.bfloat16)
    grad_pre = (upstream * upper * sigma * (1.0 + gate * (1.0 - sigma))).astype(jnp.bfloat16)
    grad_lin = (upstream * silu_gate).astype(jnp.bfloat16)
    return (grad_pre, grad_lin, activated)


def contract_rows(left, right):
    return lax.dot_general(
        left, right, (((0,), (0,)), ((), ())), preferred_element_type=jnp.float32
    )


def exchange(parts, num_dp):
    return lax.psum_scatter(parts, "dp", scatter_dimension=0, tiled=True)


def shards(
    activations, cotangent, route_ids, route_weights, gate_weights, up_weights, down_weights
):
    tok_rows, width = activations.shape
    topk = route_ids.shape[1]
    num_dp = lax.axis_size("dp")
    num_exp = lax.axis_size("expert")
    slice_width = gate_weights.shape[1]
    hidden = gate_weights.shape[2]
    capacity = min(tok_rows, 5 * tok_rows * topk // (4 * num_exp))
    flat_ids = route_ids.reshape(-1)
    expert_iota = jnp.arange(num_exp, dtype=jnp.int32)
    onehot = (flat_ids[:, None] == expert_iota[None, :]).astype(jnp.int32)
    before = jnp.cumsum(onehot, axis=0) - onehot
    slot = jnp.sum(before * onehot, axis=1)
    target = (flat_ids * capacity + slot).reshape(tok_rows, topk)
    slot_iota = jnp.arange(num_exp * capacity, dtype=jnp.int32)
    matches = target[:, :, None] == slot_iota[None, None, :]
    placing = jnp.any(matches, axis=1).astype(jnp.bfloat16)
    slot_weight = jnp.sum(jnp.where(matches, route_weights[:, :, None], 0.0), axis=(0, 1))
    by_slice = lambda a: jnp.swapaxes(a.reshape(tok_rows, num_dp, slice_width), 0, 1)
    both = jnp.concatenate([by_slice(activations), by_slice(cotangent)], axis=2)
    slots = placing.T.reshape(num_exp, capacity, tok_rows)
    scale = slot_weight.reshape(num_exp, capacity)
    gate_local = gate_weights[0]
    up_local = up_weights[0]
    down_local = down_weights[0]
    axes = ("dp", "expert")
    split = (capacity + 1) // 2
    bounds = [(0, split), (split, capacity)]
    sums = [None, None, None]
    pieces = []
    for lo, hi in bounds:
        take = hi - lo
        rows = num_exp * take
        pick = jnp.broadcast_to(slots[:, lo:hi].reshape(1, rows, tok_rows), (num_dp, rows, tok_rows))
        gathered_rows = lax.dot_general(
            pick, both, (((2,), (1,)), ((0,), (0,))), preferred_element_type=jnp.float32
        )
        weight = jnp.concatenate(
            [
                jnp.ones((rows, slice_width), jnp.float32),
                jnp.broadcast_to(scale[:, lo:hi].reshape(rows, 1), (rows, slice_width)),
            ],
            axis=1,
        )
        flat_both = (gathered_rows * weight[None]).astype(jnp.bfloat16)
        flat_both = flat_both.reshape(num_dp * num_exp, take, 2 * slice_width)
        recv_both = lax.all_to_all(flat_both, axes, split_axis=0, concat_axis=0, tiled=True)
        recv_both = recv_both.reshape(num_exp * num_dp * take, 2 * slice_width)
        act_rows = recv_both[:, :slice_width]
        cot_rows = recv_both[:, slice_width:]
        gate_part = jnp.dot(act_rows, gate_local, preferred_element_type=jnp.float32)
        up_part = jnp.dot(act_rows, up_local, preferred_element_type=jnp.float32)
        back_part = lax.dot_general(
            cot_rows, down_local, (((1,), (1,)), ((), ())), preferred_element_type=jnp.float32
        )
        summed = exchange(jnp.concatenate([gate_part, up_part, back_part], axis=1), num_dp)
        grad_pre, grad_lin, activated = swiglu_back(
            summed[:, :hidden], summed[:, hidden : 2 * hidden], summed[:, 2 * hidden :]
        )
        gathered = lax.all_gather(
            jnp.concatenate([grad_pre, grad_lin, activated], axis=1), "dp", axis=0, tiled=True
        )
        grad_pre = gathered[:, :hidden]
        grad_lin = gathered[:, hidden : 2 * hidden]
        activated = gathered[:, 2 * hidden :]
        rows_back = lax.dot_general(
            grad_pre, gate_local, (((1,), (1,)), ((), ())), preferred_element_type=jnp.float32
        ) + lax.dot_general(
            grad_lin, up_local, (((1,), (1,)), ((), ())), preferred_element_type=jnp.float32
        )
        terms = (
            contract_rows(act_rows, grad_pre),
            contract_rows(act_rows, grad_lin),
            contract_rows(activated, cot_rows),
        )
        sums = [t if s is None else s + t for s, t in zip(sums, terms)]
        flat_back = rows_back.astype(jnp.bfloat16).reshape(num_dp * num_exp, take, slice_width)
        arrived = lax.all_to_all(flat_back, axes, split_axis=0, concat_axis=0, tiled=True)
        pieces.append(arrived.reshape(num_dp, num_exp, take, slice_width))
    grad_gate, grad_up, grad_down = (s.astype(jnp.bfloat16)[None] for s in sums)
    arrived = jnp.concatenate(pieces, axis=2).reshape(num_dp, num_exp * capacity, slice_width)
    spread = jnp.broadcast_to(placing[None], (num_dp,) + placing.shape)
    grad_slices = lax.dot_general(
        spread, arrived, (((2,), (1,)), ((0,), (0,))), preferred_element_type=jnp.float32
    ).astype(jnp.bfloat16)
    grad_input = jnp.swapaxes(grad_slices, 0, 1).reshape(tok_rows, width)
    return (grad_input, grad_gate, grad_up, grad_down)


def solution(mesh):
    placed = (
        P(("expert", "dp"), None),
        P(("expert", "dp"), None),
        P(("expert", "dp"), None),
        P(("expert", "dp"), None),
        P("expert", "dp", None),
        P("expert", "dp", None),
        P("expert", None, "dp"),
    )
    return jax.shard_map(
        shards,
        mesh=mesh,
        in_specs=placed,
        out_specs=(
            P(("expert", "dp"), None),
            P("expert", "dp", None),
            P("expert", "dp", None),
            P("expert", None, "dp"),
        ),
        check_vma=False,
    )
```

```python
import jax
import jax.numpy as jnp
from jax import lax
from jax.sharding import PartitionSpec as P


def swiglu_back(gate, upper, upstream):
    sigma = jax.nn.sigmoid(gate)
    silu_gate = gate * sigma
    activated = (silu_gate * upper).astype(jnp.bfloat16)
    grad_pre = (upstream * upper * sigma * (1.0 + gate * (1.0 - sigma))).astype(jnp.bfloat16)
    grad_lin = (upstream * silu_gate).astype(jnp.bfloat16)
    return (grad_pre, grad_lin, activated)


def contract_rows(left, right):
    return lax.dot_general(
        left, right, (((0,), (0,)), ((), ())), preferred_element_type=jnp.float32
    )


def exchange(parts, num_dp):
    rows, cols = parts.shape
    parts = parts.reshape(num_dp, rows // num_dp, cols)
    me = lax.axis_index("dp")
    summed = lax.dynamic_index_in_dim(parts, me, 0, keepdims=False)
    for shift in range(1, num_dp):
        block = lax.dynamic_index_in_dim(parts, (me + shift) % num_dp, 0, keepdims=False)
        pairs = [(i, (i + shift) % num_dp) for i in range(num_dp)]
        came = lax.ppermute(block.astype(jnp.bfloat16), "dp", pairs)
        summed = summed + came.astype(jnp.float32)
    return summed


def shards(
    activations, cotangent, route_ids, route_weights, gate_weights, up_weights, down_weights
):
    tok_rows, width = activations.shape
    topk = route_ids.shape[1]
    num_dp = lax.axis_size("dp")
    num_exp = lax.axis_size("expert")
    slice_width = gate_weights.shape[1]
    hidden = gate_weights.shape[2]
    capacity = min(tok_rows, 5 * tok_rows * topk // (4 * num_exp))
    flat_ids = route_ids.reshape(-1)
    expert_iota = jnp.arange(num_exp, dtype=jnp.int32)
    onehot = (flat_ids[:, None] == expert_iota[None, :]).astype(jnp.int32)
    before = jnp.cumsum(onehot, axis=0) - onehot
    slot = jnp.sum(before * onehot, axis=1)
    target = (flat_ids * capacity + slot).reshape(tok_rows, topk)
    slot_iota = jnp.arange(num_exp * capacity, dtype=jnp.int32)
    matches = target[:, :, None] == slot_iota[None, None, :]
    placing = jnp.any(matches, axis=1).astype(jnp.bfloat16)
    slot_weight = jnp.sum(jnp.where(matches, route_weights[:, :, None], 0.0), axis=(0, 1))
    by_slice = lambda a: jnp.swapaxes(a.reshape(tok_rows, num_dp, slice_width), 0, 1)
    both = jnp.concatenate([by_slice(activations), by_slice(cotangent)], axis=2)
    slots = placing.T.reshape(num_exp, capacity, tok_rows)
    scale = slot_weight.reshape(num_exp, capacity)
    gate_local = gate_weights[0]
    up_local = up_weights[0]
    down_local = down_weights[0]
    axes = ("dp", "expert")
    split = (capacity + 1) // 2
    bounds = [(0, split), (split, capacity)]
    sums = [None, None, None]
    pieces = []
    for lo, hi in bounds:
        take = hi - lo
        rows = num_exp * take
        pick = jnp.broadcast_to(slots[:, lo:hi].reshape(1, rows, tok_rows), (num_dp, rows, tok_rows))
        gathered_rows = lax.dot_general(
            pick, both, (((2,), (1,)), ((0,), (0,))), preferred_element_type=jnp.float32
        )
        weight = jnp.concatenate(
            [
                jnp.ones((rows, slice_width), jnp.float32),
                jnp.broadcast_to(scale[:, lo:hi].reshape(rows, 1), (rows, slice_width)),
            ],
            axis=1,
        )
        flat_both = (gathered_rows * weight[None]).astype(jnp.bfloat16)
        flat_both = flat_both.reshape(num_dp * num_exp, take, 2 * slice_width)
        recv_both = lax.all_to_all(flat_both, axes, split_axis=0, concat_axis=0, tiled=True)
        recv_both = recv_both.reshape(num_exp * num_dp * take, 2 * slice_width)
        act_rows = recv_both[:, :slice_width]
        cot_rows = recv_both[:, slice_width:]
        gate_part = jnp.dot(act_rows, gate_local, preferred_element_type=jnp.float32)
        up_part = jnp.dot(act_rows, up_local, preferred_element_type=jnp.float32)
        back_part = lax.dot_general(
            cot_rows, down_local, (((1,), (1,)), ((), ())), preferred_element_type=jnp.float32
        )
        summed = exchange(jnp.concatenate([gate_part, up_part, back_part], axis=1), num_dp)
        grad_pre, grad_lin, activated = swiglu_back(
            summed[:, :hidden], summed[:, hidden : 2 * hidden], summed[:, 2 * hidden :]
        )
        gathered = lax.all_gather(
            jnp.concatenate([grad_pre, grad_lin, activated], axis=1), "dp", axis=0, tiled=True
        )
        grad_pre = gathered[:, :hidden]
        grad_lin = gathered[:, hidden : 2 * hidden]
        activated = gathered[:, 2 * hidden :]
        rows_back = lax.dot_general(
            grad_pre, gate_local, (((1,), (1,)), ((), ())), preferred_element_type=jnp.float32
        ) + lax.dot_general(
            grad_lin, up_local, (((1,), (1,)), ((), ())), preferred_element_type=jnp.float32
        )
        terms = (
            contract_rows(act_rows, grad_pre),
            contract_rows(act_rows, grad_lin),
            contract_rows(activated, cot_rows),
        )
        sums = [t if s is None else s + t for s, t in zip(sums, terms)]
        flat_back = rows_back.astype(jnp.bfloat16).reshape(num_dp * num_exp, take, slice_width)
        arrived = lax.all_to_all(flat_back, axes, split_axis=0, concat_axis=0, tiled=True)
        pieces.append(arrived.reshape(num_dp, num_exp, take, slice_width))
    grad_gate, grad_up, grad_down = (s.astype(jnp.bfloat16)[None] for s in sums)
    arrived = jnp.concatenate(pieces, axis=2).reshape(num_dp, num_exp * capacity, slice_width)
    spread = jnp.broadcast_to(placing[None], (num_dp,) + placing.shape)
    grad_slices = lax.dot_general(
        spread, arrived, (((2,), (1,)), ((0,), (0,))), preferred_element_type=jnp.float32
    ).astype(jnp.bfloat16)
    grad_input = jnp.swapaxes(grad_slices, 0, 1).reshape(tok_rows, width)
    return (grad_input, grad_gate, grad_up, grad_down)


def solution(mesh):
    placed = (
        P(("expert", "dp"), None),
        P(("expert", "dp"), None),
        P(("expert", "dp"), None),
        P(("expert", "dp"), None),
        P("expert", "dp", None),
        P("expert", "dp", None),
        P("expert", None, "dp"),
    )
    return jax.shard_map(
        shards,
        mesh=mesh,
        in_specs=placed,
        out_specs=(
            P(("expert", "dp"), None),
            P("expert", "dp", None),
            P("expert", "dp", None),
            P("expert", None, "dp"),
        ),
        check_vma=False,
    )
```

```python
import jax
import jax.numpy as jnp
from jax import lax
from jax.sharding import PartitionSpec as P


def swiglu_back(gate, upper, upstream):
    sigma = jax.nn.sigmoid(gate)
    silu_gate = gate * sigma
    activated = (silu_gate * upper).astype(jnp.bfloat16)
    grad_pre = (upstream * upper * sigma * (1.0 + gate * (1.0 - sigma))).astype(jnp.bfloat16)
    grad_lin = (upstream * silu_gate).astype(jnp.bfloat16)
    return (grad_pre, grad_lin, activated)


def contract_rows(left, right):
    return lax.dot_general(
        left, right, (((0,), (0,)), ((), ())), preferred_element_type=jnp.float32
    )


def exchange(parts, num_dp):
    rows, cols = parts.shape
    parts = parts.reshape(num_dp, rows // num_dp, cols)
    me = lax.axis_index("dp")
    half = cols // 2
    block = lambda k: lax.dynamic_index_in_dim(
        parts, (me + k) % num_dp, 0, keepdims=False
    ).astype(jnp.bfloat16)
    up = [(i, (i + 1) % num_dp) for i in range(num_dp)]
    down = [(i, (i - 1) % num_dp) for i in range(num_dp)]
    far = block(2)
    from_down = lax.ppermute(jnp.concatenate([block(1), far[:, :half]], axis=1), "dp", up)
    from_up = lax.ppermute(jnp.concatenate([block(-1), far[:, half:]], axis=1), "dp", down)
    far_lo = lax.ppermute(from_down[:, cols:], "dp", up)
    far_hi = lax.ppermute(from_up[:, cols:], "dp", down)
    own = lax.dynamic_index_in_dim(parts, me, 0, keepdims=False)
    far_sum = jnp.concatenate([far_lo, far_hi], axis=1).astype(jnp.float32)
    return (
        own
        + from_down[:, :cols].astype(jnp.float32)
        + from_up[:, :cols].astype(jnp.float32)
        + far_sum
    )


def gather_dp(piece, num_dp):
    rows, cols = piece.shape
    me = lax.axis_index("dp")
    half = cols // 2
    up = [(i, (i + 1) % num_dp) for i in range(num_dp)]
    down = [(i, (i - 1) % num_dp) for i in range(num_dp)]
    from_down = lax.ppermute(piece, "dp", up)
    from_up = lax.ppermute(piece, "dp", down)
    far_lo = lax.ppermute(from_down[:, :half], "dp", up)
    far_hi = lax.ppermute(from_up[:, half:], "dp", down)
    far = jnp.concatenate([far_lo, far_hi], axis=1)
    out = jnp.zeros((num_dp, rows, cols), piece.dtype)
    for k, value in ((0, piece), (1, from_up), (2, far), (num_dp - 1, from_down)):
        out = lax.dynamic_update_index_in_dim(out, value, (me + k) % num_dp, 0)
    return out.reshape(num_dp * rows, cols)


def shards(
    activations, cotangent, route_ids, route_weights, gate_weights, up_weights, down_weights
):
    tok_rows, width = activations.shape
    topk = route_ids.shape[1]
    num_dp = lax.axis_size("dp")
    num_exp = lax.axis_size("expert")
    slice_width = gate_weights.shape[1]
    hidden = gate_weights.shape[2]
    capacity = min(tok_rows, 5 * tok_rows * topk // (4 * num_exp))
    flat_ids = route_ids.reshape(-1)
    expert_iota = jnp.arange(num_exp, dtype=jnp.int32)
    onehot = (flat_ids[:, None] == expert_iota[None, :]).astype(jnp.int32)
    before = jnp.cumsum(onehot, axis=0) - onehot
    slot = jnp.sum(before * onehot, axis=1)
    target = (flat_ids * capacity + slot).reshape(tok_rows, topk)
    slot_iota = jnp.arange(num_exp * capacity, dtype=jnp.int32)
    matches = target[:, :, None] == slot_iota[None, None, :]
    placing = jnp.any(matches, axis=1).astype(jnp.bfloat16)
    slot_weight = jnp.sum(jnp.where(matches, route_weights[:, :, None], 0.0), axis=(0, 1))
    by_slice = lambda a: jnp.swapaxes(a.reshape(tok_rows, num_dp, slice_width), 0, 1)
    both = jnp.concatenate([by_slice(activations), by_slice(cotangent)], axis=2)
    slots = placing.T.reshape(num_exp, capacity, tok_rows)
    scale = slot_weight.reshape(num_exp, capacity)
    gate_local = gate_weights[0]
    up_local = up_weights[0]
    down_local = down_weights[0]
    axes = ("dp", "expert")
    split = (capacity + 1) // 2
    bounds = [(0, split), (split, capacity)]
    sums = [None, None, None]
    pieces = []
    for lo, hi in bounds:
        take = hi - lo
        rows = num_exp * take
        pick = jnp.broadcast_to(slots[:, lo:hi].reshape(1, rows, tok_rows), (num_dp, rows, tok_rows))
        gathered_rows = lax.dot_general(
            pick, both, (((2,), (1,)), ((0,), (0,))), preferred_element_type=jnp.float32
        )
        weight = jnp.concatenate(
            [
                jnp.ones((rows, slice_width), jnp.float32),
                jnp.broadcast_to(scale[:, lo:hi].reshape(rows, 1), (rows, slice_width)),
            ],
            axis=1,
        )
        flat_both = (gathered_rows * weight[None]).astype(jnp.bfloat16)
        flat_both = flat_both.reshape(num_dp * num_exp, take, 2 * slice_width)
        recv_both = lax.all_to_all(flat_both, axes, split_axis=0, concat_axis=0, tiled=True)
        recv_both = recv_both.reshape(num_exp * num_dp * take, 2 * slice_width)
        act_rows = recv_both[:, :slice_width]
        cot_rows = recv_both[:, slice_width:]
        gate_part = jnp.dot(act_rows, gate_local, preferred_element_type=jnp.float32)
        up_part = jnp.dot(act_rows, up_local, preferred_element_type=jnp.float32)
        back_part = lax.dot_general(
            cot_rows, down_local, (((1,), (1,)), ((), ())), preferred_element_type=jnp.float32
        )
        summed = exchange(jnp.concatenate([gate_part, up_part, back_part], axis=1), num_dp)
        grad_pre, grad_lin, activated = swiglu_back(
            summed[:, :hidden], summed[:, hidden : 2 * hidden], summed[:, 2 * hidden :]
        )
        gathered = gather_dp(jnp.concatenate([grad_pre, grad_lin, activated], axis=1), num_dp)
        grad_pre = gathered[:, :hidden]
        grad_lin = gathered[:, hidden : 2 * hidden]
        activated = gathered[:, 2 * hidden :]
        rows_back = lax.dot_general(
            grad_pre, gate_local, (((1,), (1,)), ((), ())), preferred_element_type=jnp.float32
        ) + lax.dot_general(
            grad_lin, up_local, (((1,), (1,)), ((), ())), preferred_element_type=jnp.float32
        )
        terms = (
            contract_rows(act_rows, grad_pre),
            contract_rows(act_rows, grad_lin),
            contract_rows(activated, cot_rows),
        )
        sums = [t if s is None else s + t for s, t in zip(sums, terms)]
        flat_back = rows_back.astype(jnp.bfloat16).reshape(num_dp * num_exp, take, slice_width)
        arrived = lax.all_to_all(flat_back, axes, split_axis=0, concat_axis=0, tiled=True)
        pieces.append(arrived.reshape(num_dp, num_exp, take, slice_width))
    grad_gate, grad_up, grad_down = (s.astype(jnp.bfloat16)[None] for s in sums)
    arrived = jnp.concatenate(pieces, axis=2).reshape(num_dp, num_exp * capacity, slice_width)
    spread = jnp.broadcast_to(placing[None], (num_dp,) + placing.shape)
    grad_slices = lax.dot_general(
        spread, arrived, (((2,), (1,)), ((0,), (0,))), preferred_element_type=jnp.float32
    ).astype(jnp.bfloat16)
    grad_input = jnp.swapaxes(grad_slices, 0, 1).reshape(tok_rows, width)
    return (grad_input, grad_gate, grad_up, grad_down)


def solution(mesh):
    placed = (
        P(("expert", "dp"), None),
        P(("expert", "dp"), None),
        P(("expert", "dp"), None),
        P(("expert", "dp"), None),
        P("expert", "dp", None),
        P("expert", "dp", None),
        P("expert", None, "dp"),
    )
    return jax.shard_map(
        shards,
        mesh=mesh,
        in_specs=placed,
        out_specs=(
            P(("expert", "dp"), None),
            P("expert", "dp", None),
            P("expert", "dp", None),
            P("expert", None, "dp"),
        ),
        check_vma=False,
    )
```

```python
import jax
import jax.numpy as jnp
from jax import lax
from jax.sharding import PartitionSpec as P


def swiglu_back(gate, upper, upstream):
    sigma = jax.nn.sigmoid(gate)
    silu_gate = gate * sigma
    activated = (silu_gate * upper).astype(jnp.bfloat16)
    grad_pre = (upstream * upper * sigma * (1.0 + gate * (1.0 - sigma))).astype(jnp.bfloat16)
    grad_lin = (upstream * silu_gate).astype(jnp.bfloat16)
    return (grad_pre, grad_lin, activated)


def contract_rows(left, right):
    return lax.dot_general(
        left, right, (((0,), (0,)), ((), ())), preferred_element_type=jnp.float32
    )


def exchange(parts, num_dp):
    rows, cols = parts.shape
    parts = parts.reshape(num_dp, rows // num_dp, cols)
    me = lax.axis_index("dp")
    half = cols // 2
    block = lambda k: lax.dynamic_index_in_dim(
        parts, (me + k) % num_dp, 0, keepdims=False
    ).astype(jnp.bfloat16)
    up = [(i, (i + 1) % num_dp) for i in range(num_dp)]
    down = [(i, (i - 1) % num_dp) for i in range(num_dp)]
    far = block(2)
    from_down = lax.ppermute(jnp.concatenate([block(1), far[:, :half]], axis=1), "dp", up)
    from_up = lax.ppermute(jnp.concatenate([block(-1), far[:, half:]], axis=1), "dp", down)
    far_lo = lax.ppermute(from_down[:, cols:], "dp", up)
    far_hi = lax.ppermute(from_up[:, cols:], "dp", down)
    own = lax.dynamic_index_in_dim(parts, me, 0, keepdims=False)
    far_sum = jnp.concatenate([far_lo, far_hi], axis=1).astype(jnp.float32)
    return (
        own
        + from_down[:, :cols].astype(jnp.float32)
        + from_up[:, :cols].astype(jnp.float32)
        + far_sum
    )


def shards(
    activations, cotangent, route_ids, route_weights, gate_weights, up_weights, down_weights
):
    tok_rows, width = activations.shape
    topk = route_ids.shape[1]
    num_dp = lax.axis_size("dp")
    num_exp = lax.axis_size("expert")
    slice_width = gate_weights.shape[1]
    hidden = gate_weights.shape[2]
    capacity = min(tok_rows, 5 * tok_rows * topk // (4 * num_exp))
    flat_ids = route_ids.reshape(-1)
    expert_iota = jnp.arange(num_exp, dtype=jnp.int32)
    onehot = (flat_ids[:, None] == expert_iota[None, :]).astype(jnp.int32)
    before = jnp.cumsum(onehot, axis=0) - onehot
    slot = jnp.sum(before * onehot, axis=1)
    target = (flat_ids * capacity + slot).reshape(tok_rows, topk)
    slot_iota = jnp.arange(num_exp * capacity, dtype=jnp.int32)
    matches = target[:, :, None] == slot_iota[None, None, :]
    placing = jnp.any(matches, axis=1).astype(jnp.bfloat16)
    slot_weight = jnp.sum(jnp.where(matches, route_weights[:, :, None], 0.0), axis=(0, 1))
    by_slice = lambda a: jnp.swapaxes(a.reshape(tok_rows, num_dp, slice_width), 0, 1)
    both = jnp.concatenate([by_slice(activations), by_slice(cotangent)], axis=2)
    slots = placing.T.reshape(num_exp, capacity, tok_rows)
    scale = slot_weight.reshape(num_exp, capacity)
    gate_local = gate_weights[0]
    up_local = up_weights[0]
    down_local = down_weights[0]
    axes = ("dp", "expert")
    split = (capacity + 1) // 2
    bounds = [(0, split), (split, capacity)]
    sums = [None, None, None]
    pieces = []
    for lo, hi in bounds:
        take = hi - lo
        rows = num_exp * take
        pick = jnp.broadcast_to(slots[:, lo:hi].reshape(1, rows, tok_rows), (num_dp, rows, tok_rows))
        gathered_rows = lax.dot_general(
            pick, both, (((2,), (1,)), ((0,), (0,))), preferred_element_type=jnp.float32
        )
        weight = jnp.concatenate(
            [
                jnp.ones((rows, slice_width), jnp.float32),
                jnp.broadcast_to(scale[:, lo:hi].reshape(rows, 1), (rows, slice_width)),
            ],
            axis=1,
        )
        flat_both = (gathered_rows * weight[None]).astype(jnp.bfloat16)
        flat_both = flat_both.reshape(num_dp * num_exp, take, 2 * slice_width)
        recv_both = lax.all_to_all(flat_both, axes, split_axis=0, concat_axis=0, tiled=True)
        recv_both = recv_both.reshape(num_exp * num_dp * take, 2 * slice_width)
        act_rows = recv_both[:, :slice_width]
        cot_rows = recv_both[:, slice_width:]
        gate_part = jnp.dot(act_rows, gate_local, preferred_element_type=jnp.float32)
        up_part = jnp.dot(act_rows, up_local, preferred_element_type=jnp.float32)
        back_part = lax.dot_general(
            cot_rows, down_local, (((1,), (1,)), ((), ())), preferred_element_type=jnp.float32
        )
        summed = exchange(jnp.concatenate([gate_part, up_part, back_part], axis=1), num_dp)
        grad_pre, grad_lin, activated = swiglu_back(
            summed[:, :hidden], summed[:, hidden : 2 * hidden], summed[:, 2 * hidden :]
        )
        gathered = lax.all_gather(
            jnp.concatenate([grad_pre, grad_lin, activated], axis=1), "dp", axis=0, tiled=True
        )
        grad_pre = gathered[:, :hidden]
        grad_lin = gathered[:, hidden : 2 * hidden]
        activated = gathered[:, 2 * hidden :]
        rows_back = lax.dot_general(
            grad_pre, gate_local, (((1,), (1,)), ((), ())), preferred_element_type=jnp.float32
        ) + lax.dot_general(
            grad_lin, up_local, (((1,), (1,)), ((), ())), preferred_element_type=jnp.float32
        )
        terms = (
            contract_rows(act_rows, grad_pre),
            contract_rows(act_rows, grad_lin),
            contract_rows(activated, cot_rows),
        )
        sums = [t if s is None else s + t for s, t in zip(sums, terms)]
        flat_back = rows_back.astype(jnp.bfloat16).reshape(num_dp * num_exp, take, slice_width)
        arrived = lax.all_to_all(flat_back, axes, split_axis=0, concat_axis=0, tiled=True)
        pieces.append(arrived.reshape(num_dp, num_exp, take, slice_width))
    grad_gate, grad_up, grad_down = (s.astype(jnp.bfloat16)[None] for s in sums)
    arrived = jnp.concatenate(pieces, axis=2).reshape(num_dp, num_exp * capacity, slice_width)
    spread = jnp.broadcast_to(placing[None], (num_dp,) + placing.shape)
    grad_slices = lax.dot_general(
        spread, arrived, (((2,), (1,)), ((0,), (0,))), preferred_element_type=jnp.float32
    ).astype(jnp.bfloat16)
    grad_input = jnp.swapaxes(grad_slices, 0, 1).reshape(tok_rows, width)
    return (grad_input, grad_gate, grad_up, grad_down)


def solution(mesh):
    placed = (
        P(("expert", "dp"), None),
        P(("expert", "dp"), None),
        P(("expert", "dp"), None),
        P(("expert", "dp"), None),
        P("expert", "dp", None),
        P("expert", "dp", None),
        P("expert", None, "dp"),
    )
    return jax.shard_map(
        shards,
        mesh=mesh,
        in_specs=placed,
        out_specs=(
            P(("expert", "dp"), None),
            P("expert", "dp", None),
            P("expert", "dp", None),
            P("expert", None, "dp"),
        ),
        check_vma=False,
    )
```

```python
import jax
import jax.numpy as jnp
from jax import lax
from jax.sharding import PartitionSpec as P


def swiglu_back(gate, upper, upstream):
    sigma = jax.nn.sigmoid(gate)
    silu_gate = gate * sigma
    activated = (silu_gate * upper).astype(jnp.bfloat16)
    grad_pre = (upstream * upper * sigma * (1.0 + gate * (1.0 - sigma))).astype(jnp.bfloat16)
    grad_lin = (upstream * silu_gate).astype(jnp.bfloat16)
    return (grad_pre, grad_lin, activated)


def contract_rows(left, right):
    return lax.dot_general(
        left, right, (((0,), (0,)), ((), ())), preferred_element_type=jnp.float32
    )


def exchange(parts, num_dp):
    rows, cols = parts.shape
    parts = parts.reshape(num_dp, rows // num_dp, cols)
    me = lax.axis_index("dp")
    summed = lax.dynamic_index_in_dim(parts, me, 0, keepdims=False)
    for shift in range(1, num_dp):
        block = lax.dynamic_index_in_dim(parts, (me + shift) % num_dp, 0, keepdims=False)
        pairs = [(i, (i + shift) % num_dp) for i in range(num_dp)]
        came = lax.ppermute(block.astype(jnp.bfloat16), "dp", pairs)
        summed = summed + came.astype(jnp.float32)
    return summed


def shards(
    activations, cotangent, route_ids, route_weights, gate_weights, up_weights, down_weights
):
    tok_rows, width = activations.shape
    topk = route_ids.shape[1]
    num_dp = lax.axis_size("dp")
    num_exp = lax.axis_size("expert")
    slice_width = gate_weights.shape[1]
    hidden = gate_weights.shape[2]
    capacity = min(tok_rows, 5 * tok_rows * topk // (4 * num_exp))
    flat_ids = route_ids.reshape(-1)
    expert_iota = jnp.arange(num_exp, dtype=jnp.int32)
    onehot = (flat_ids[:, None] == expert_iota[None, :]).astype(jnp.int32)
    before = jnp.cumsum(onehot, axis=0) - onehot
    slot = jnp.sum(before * onehot, axis=1)
    target = (flat_ids * capacity + slot).reshape(tok_rows, topk)
    slot_iota = jnp.arange(num_exp * capacity, dtype=jnp.int32)
    matches = target[:, :, None] == slot_iota[None, None, :]
    placing = jnp.any(matches, axis=1).astype(jnp.bfloat16)
    slot_weight = jnp.sum(jnp.where(matches, route_weights[:, :, None], 0.0), axis=(0, 1))
    by_slice = lambda a: jnp.swapaxes(a.reshape(tok_rows, num_dp, slice_width), 0, 1)
    both = jnp.concatenate([by_slice(activations), by_slice(cotangent)], axis=2)
    slots = placing.T.reshape(num_exp, capacity, tok_rows)
    scale = slot_weight.reshape(num_exp, capacity)
    gate_local = gate_weights[0]
    up_local = up_weights[0]
    down_local = down_weights[0]
    axes = ("dp", "expert")
    split = (capacity + 1) // 2
    bounds = [(0, split), (split, capacity)]
    sums = [None, None, None]
    pieces = []
    for lo, hi in bounds:
        take = hi - lo
        rows = num_exp * take
        pick = jnp.broadcast_to(slots[:, lo:hi].reshape(1, rows, tok_rows), (num_dp, rows, tok_rows))
        gathered_rows = lax.dot_general(
            pick, both, (((2,), (1,)), ((0,), (0,))), preferred_element_type=jnp.float32
        )
        weight = jnp.concatenate(
            [
                jnp.ones((rows, slice_width), jnp.float32),
                jnp.broadcast_to(scale[:, lo:hi].reshape(rows, 1), (rows, slice_width)),
            ],
            axis=1,
        )
        flat_both = (gathered_rows * weight[None]).astype(jnp.bfloat16)
        flat_both = flat_both.reshape(num_dp * num_exp, take, 2 * slice_width)
        if pieces:
            _, flat_both = lax.optimization_barrier((recv_prev, flat_both))
        recv_both = lax.all_to_all(flat_both, axes, split_axis=0, concat_axis=0, tiled=True)
        recv_prev = recv_both
        recv_both = recv_both.reshape(num_exp * num_dp * take, 2 * slice_width)
        act_rows = recv_both[:, :slice_width]
        cot_rows = recv_both[:, slice_width:]
        gate_part = jnp.dot(act_rows, gate_local, preferred_element_type=jnp.float32)
        up_part = jnp.dot(act_rows, up_local, preferred_element_type=jnp.float32)
        back_part = lax.dot_general(
            cot_rows, down_local, (((1,), (1,)), ((), ())), preferred_element_type=jnp.float32
        )
        summed = exchange(jnp.concatenate([gate_part, up_part, back_part], axis=1), num_dp)
        grad_pre, grad_lin, activated = swiglu_back(
            summed[:, :hidden], summed[:, hidden : 2 * hidden], summed[:, 2 * hidden :]
        )
        gathered = lax.all_gather(
            jnp.concatenate([grad_pre, grad_lin, activated], axis=1), "dp", axis=0, tiled=True
        )
        grad_pre = gathered[:, :hidden]
        grad_lin = gathered[:, hidden : 2 * hidden]
        activated = gathered[:, 2 * hidden :]
        rows_back = lax.dot_general(
            grad_pre, gate_local, (((1,), (1,)), ((), ())), preferred_element_type=jnp.float32
        ) + lax.dot_general(
            grad_lin, up_local, (((1,), (1,)), ((), ())), preferred_element_type=jnp.float32
        )
        terms = (
            contract_rows(act_rows, grad_pre),
            contract_rows(act_rows, grad_lin),
            contract_rows(activated, cot_rows),
        )
        sums = [t if s is None else s + t for s, t in zip(sums, terms)]
        flat_back = rows_back.astype(jnp.bfloat16).reshape(num_dp * num_exp, take, slice_width)
        arrived = lax.all_to_all(flat_back, axes, split_axis=0, concat_axis=0, tiled=True)
        pieces.append(arrived.reshape(num_dp, num_exp, take, slice_width))
    grad_gate, grad_up, grad_down = (s.astype(jnp.bfloat16)[None] for s in sums)
    arrived = jnp.concatenate(pieces, axis=2).reshape(num_dp, num_exp * capacity, slice_width)
    spread = jnp.broadcast_to(placing[None], (num_dp,) + placing.shape)
    grad_slices = lax.dot_general(
        spread, arrived, (((2,), (1,)), ((0,), (0,))), preferred_element_type=jnp.float32
    ).astype(jnp.bfloat16)
    grad_input = jnp.swapaxes(grad_slices, 0, 1).reshape(tok_rows, width)
    return (grad_input, grad_gate, grad_up, grad_down)


def solution(mesh):
    placed = (
        P(("expert", "dp"), None),
        P(("expert", "dp"), None),
        P(("expert", "dp"), None),
        P(("expert", "dp"), None),
        P("expert", "dp", None),
        P("expert", "dp", None),
        P("expert", None, "dp"),
    )
    return jax.shard_map(
        shards,
        mesh=mesh,
        in_specs=placed,
        out_specs=(
            P(("expert", "dp"), None),
            P("expert", "dp", None),
            P("expert", "dp", None),
            P("expert", None, "dp"),
        ),
        check_vma=False,
    )
```

```python
import jax
import jax.numpy as jnp
from jax import lax
from jax.sharding import PartitionSpec as P


def swiglu_back(gate, upper, upstream):
    sigma = jax.nn.sigmoid(gate)
    silu_gate = gate * sigma
    activated = (silu_gate * upper).astype(jnp.bfloat16)
    grad_pre = (upstream * upper * sigma * (1.0 + gate * (1.0 - sigma))).astype(jnp.bfloat16)
    grad_lin = (upstream * silu_gate).astype(jnp.bfloat16)
    return (grad_pre, grad_lin, activated)


def contract_rows(left, right):
    return lax.dot_general(
        left, right, (((0,), (0,)), ((), ())), preferred_element_type=jnp.float32
    )


def exchange(parts, num_dp):
    rows, cols = parts.shape
    parts = parts.reshape(num_dp, rows // num_dp, cols)
    me = lax.axis_index("dp")
    summed = lax.dynamic_index_in_dim(parts, me, 0, keepdims=False)
    for shift in range(1, num_dp):
        block = lax.dynamic_index_in_dim(parts, (me + shift) % num_dp, 0, keepdims=False)
        pairs = [(i, (i + shift) % num_dp) for i in range(num_dp)]
        came = lax.ppermute(block.astype(jnp.bfloat16), "dp", pairs)
        summed = summed + came.astype(jnp.float32)
    return summed


def shards(
    activations, cotangent, route_ids, route_weights, gate_weights, up_weights, down_weights
):
    tok_rows, width = activations.shape
    topk = route_ids.shape[1]
    num_dp = lax.axis_size("dp")
    num_exp = lax.axis_size("expert")
    slice_width = gate_weights.shape[1]
    hidden = gate_weights.shape[2]
    capacity = min(tok_rows, 5 * tok_rows * topk // (4 * num_exp))
    flat_ids = route_ids.reshape(-1)
    expert_iota = jnp.arange(num_exp, dtype=jnp.int32)
    onehot = (flat_ids[:, None] == expert_iota[None, :]).astype(jnp.int32)
    before = jnp.cumsum(onehot, axis=0) - onehot
    slot = jnp.sum(before * onehot, axis=1)
    target = (flat_ids * capacity + slot).reshape(tok_rows, topk)
    slot_iota = jnp.arange(num_exp * capacity, dtype=jnp.int32)
    matches = target[:, :, None] == slot_iota[None, None, :]
    placing = jnp.any(matches, axis=1).astype(jnp.bfloat16)
    slot_weight = jnp.sum(jnp.where(matches, route_weights[:, :, None], 0.0), axis=(0, 1))
    by_slice = lambda a: jnp.swapaxes(a.reshape(tok_rows, num_dp, slice_width), 0, 1)
    both = jnp.concatenate([by_slice(activations), by_slice(cotangent)], axis=2)
    slots = placing.T.reshape(num_exp, capacity, tok_rows)
    scale = slot_weight.reshape(num_exp, capacity)
    gate_local = gate_weights[0]
    up_local = up_weights[0]
    down_local = down_weights[0]
    axes = ("dp", "expert")
    split = (capacity + 1) // 2
    bounds = [(0, split), (split, capacity)]
    sums = [None, None, None]
    pieces = []
    for lo, hi in bounds:
        take = hi - lo
        rows = num_exp * take
        pick = jnp.broadcast_to(slots[:, lo:hi].reshape(1, rows, tok_rows), (num_dp, rows, tok_rows))
        gathered_rows = lax.dot_general(
            pick, both, (((2,), (1,)), ((0,), (0,))), preferred_element_type=jnp.float32
        )
        weight = jnp.concatenate(
            [
                jnp.ones((rows, slice_width), jnp.float32),
                jnp.broadcast_to(scale[:, lo:hi].reshape(rows, 1), (rows, slice_width)),
            ],
            axis=1,
        )
        flat_both = (gathered_rows * weight[None]).astype(jnp.bfloat16)
        flat_both = flat_both.reshape(num_dp * num_exp, take, 2 * slice_width)
        recv_both = lax.all_to_all(flat_both, axes, split_axis=0, concat_axis=0, tiled=True)
        recv_both = recv_both.reshape(num_exp * num_dp * take, 2 * slice_width)
        act_rows = recv_both[:, :slice_width]
        cot_rows = recv_both[:, slice_width:]
        gate_part = jnp.dot(act_rows, gate_local, preferred_element_type=jnp.float32)
        up_part = jnp.dot(act_rows, up_local, preferred_element_type=jnp.float32)
        back_part = lax.dot_general(
            cot_rows, down_local, (((1,), (1,)), ((), ())), preferred_element_type=jnp.float32
        )
        summed = exchange(jnp.concatenate([gate_part, up_part, back_part], axis=1), num_dp)
        grad_pre, grad_lin, activated = swiglu_back(
            summed[:, :hidden], summed[:, hidden : 2 * hidden], summed[:, 2 * hidden :]
        )
        gathered = lax.all_gather(
            jnp.concatenate([grad_pre, grad_lin], axis=1), "dp", axis=0, tiled=True
        )
        activated = lax.all_gather(activated, "dp", axis=0, tiled=True)
        grad_pre = gathered[:, :hidden]
        grad_lin = gathered[:, hidden:]
        rows_back = lax.dot_general(
            grad_pre, gate_local, (((1,), (1,)), ((), ())), preferred_element_type=jnp.float32
        ) + lax.dot_general(
            grad_lin, up_local, (((1,), (1,)), ((), ())), preferred_element_type=jnp.float32
        )
        terms = (
            contract_rows(act_rows, grad_pre),
            contract_rows(act_rows, grad_lin),
            contract_rows(activated, cot_rows),
        )
        sums = [t if s is None else s + t for s, t in zip(sums, terms)]
        flat_back = rows_back.astype(jnp.bfloat16).reshape(num_dp * num_exp, take, slice_width)
        arrived = lax.all_to_all(flat_back, axes, split_axis=0, concat_axis=0, tiled=True)
        pieces.append(arrived.reshape(num_dp, num_exp, take, slice_width))
    grad_gate, grad_up, grad_down = (s.astype(jnp.bfloat16)[None] for s in sums)
    arrived = jnp.concatenate(pieces, axis=2).reshape(num_dp, num_exp * capacity, slice_width)
    spread = jnp.broadcast_to(placing[None], (num_dp,) + placing.shape)
    grad_slices = lax.dot_general(
        spread, arrived, (((2,), (1,)), ((0,), (0,))), preferred_element_type=jnp.float32
    ).astype(jnp.bfloat16)
    grad_input = jnp.swapaxes(grad_slices, 0, 1).reshape(tok_rows, width)
    return (grad_input, grad_gate, grad_up, grad_down)


def solution(mesh):
    placed = (
        P(("expert", "dp"), None),
        P(("expert", "dp"), None),
        P(("expert", "dp"), None),
        P(("expert", "dp"), None),
        P("expert", "dp", None),
        P("expert", "dp", None),
        P("expert", None, "dp"),
    )
    return jax.shard_map(
        shards,
        mesh=mesh,
        in_specs=placed,
        out_specs=(
            P(("expert", "dp"), None),
            P("expert", "dp", None),
            P("expert", "dp", None),
            P("expert", None, "dp"),
        ),
        check_vma=False,
    )
```

```python
import jax
import jax.numpy as jnp
from jax import lax
from jax.sharding import PartitionSpec as P


def swiglu_back(gate, upper, upstream):
    sigma = jax.nn.sigmoid(gate)
    silu_gate = gate * sigma
    activated = (silu_gate * upper).astype(jnp.bfloat16)
    grad_pre = (upstream * upper * sigma * (1.0 + gate * (1.0 - sigma))).astype(jnp.bfloat16)
    grad_lin = (upstream * silu_gate).astype(jnp.bfloat16)
    return (grad_pre, grad_lin, activated)


def contract_rows(left, right):
    return lax.dot_general(
        left, right, (((0,), (0,)), ((), ())), preferred_element_type=jnp.float32
    )


def exchange_queued(parts, num_dp):
    rows, cols = parts.shape
    parts = parts.reshape(num_dp, rows // num_dp, cols)
    me = lax.axis_index("dp")
    own = lax.dynamic_index_in_dim(parts, me, 0, keepdims=False)
    came = lax.all_to_all(
        parts.astype(jnp.bfloat16), "dp", split_axis=0, concat_axis=0, tiled=True
    )
    others = (jnp.arange(num_dp, dtype=jnp.int32) != me).astype(jnp.float32)
    return own + jnp.sum(came.astype(jnp.float32) * others[:, None, None], axis=0)


def exchange(parts, num_dp):
    rows, cols = parts.shape
    parts = parts.reshape(num_dp, rows // num_dp, cols)
    me = lax.axis_index("dp")
    summed = lax.dynamic_index_in_dim(parts, me, 0, keepdims=False)
    for shift in range(1, num_dp):
        block = lax.dynamic_index_in_dim(parts, (me + shift) % num_dp, 0, keepdims=False)
        pairs = [(i, (i + shift) % num_dp) for i in range(num_dp)]
        came = lax.ppermute(block.astype(jnp.bfloat16), "dp", pairs)
        summed = summed + came.astype(jnp.float32)
    return summed


def shards(
    activations, cotangent, route_ids, route_weights, gate_weights, up_weights, down_weights
):
    tok_rows, width = activations.shape
    topk = route_ids.shape[1]
    num_dp = lax.axis_size("dp")
    num_exp = lax.axis_size("expert")
    slice_width = gate_weights.shape[1]
    hidden = gate_weights.shape[2]
    capacity = min(tok_rows, 5 * tok_rows * topk // (4 * num_exp))
    flat_ids = route_ids.reshape(-1)
    expert_iota = jnp.arange(num_exp, dtype=jnp.int32)
    onehot = (flat_ids[:, None] == expert_iota[None, :]).astype(jnp.int32)
    before = jnp.cumsum(onehot, axis=0) - onehot
    slot = jnp.sum(before * onehot, axis=1)
    target = (flat_ids * capacity + slot).reshape(tok_rows, topk)
    slot_iota = jnp.arange(num_exp * capacity, dtype=jnp.int32)
    matches = target[:, :, None] == slot_iota[None, None, :]
    placing = jnp.any(matches, axis=1).astype(jnp.bfloat16)
    slot_weight = jnp.sum(jnp.where(matches, route_weights[:, :, None], 0.0), axis=(0, 1))
    by_slice = lambda a: jnp.swapaxes(a.reshape(tok_rows, num_dp, slice_width), 0, 1)
    both = jnp.concatenate([by_slice(activations), by_slice(cotangent)], axis=2)
    slots = placing.T.reshape(num_exp, capacity, tok_rows)
    scale = slot_weight.reshape(num_exp, capacity)
    gate_local = gate_weights[0]
    up_local = up_weights[0]
    down_local = down_weights[0]
    axes = ("dp", "expert")
    split = (capacity + 1) // 2
    bounds = [(0, split), (split, capacity)]
    sums = [None, None, None]
    pieces = []
    for lo, hi in bounds:
        take = hi - lo
        rows = num_exp * take
        pick = jnp.broadcast_to(slots[:, lo:hi].reshape(1, rows, tok_rows), (num_dp, rows, tok_rows))
        gathered_rows = lax.dot_general(
            pick, both, (((2,), (1,)), ((0,), (0,))), preferred_element_type=jnp.float32
        )
        weight = jnp.concatenate(
            [
                jnp.ones((rows, slice_width), jnp.float32),
                jnp.broadcast_to(scale[:, lo:hi].reshape(rows, 1), (rows, slice_width)),
            ],
            axis=1,
        )
        flat_both = (gathered_rows * weight[None]).astype(jnp.bfloat16)
        flat_both = flat_both.reshape(num_dp * num_exp, take, 2 * slice_width)
        recv_both = lax.all_to_all(flat_both, axes, split_axis=0, concat_axis=0, tiled=True)
        recv_both = recv_both.reshape(num_exp * num_dp * take, 2 * slice_width)
        act_rows = recv_both[:, :slice_width]
        cot_rows = recv_both[:, slice_width:]
        gate_part = jnp.dot(act_rows, gate_local, preferred_element_type=jnp.float32)
        up_part = jnp.dot(act_rows, up_local, preferred_element_type=jnp.float32)
        back_part = lax.dot_general(
            cot_rows, down_local, (((1,), (1,)), ((), ())), preferred_element_type=jnp.float32
        )
        swap = exchange if lo == 0 else exchange_queued
        summed = swap(jnp.concatenate([gate_part, up_part, back_part], axis=1), num_dp)
        grad_pre, grad_lin, activated = swiglu_back(
            summed[:, :hidden], summed[:, hidden : 2 * hidden], summed[:, 2 * hidden :]
        )
        gathered = lax.all_gather(
            jnp.concatenate([grad_pre, grad_lin, activated], axis=1), "dp", axis=0, tiled=True
        )
        grad_pre = gathered[:, :hidden]
        grad_lin = gathered[:, hidden : 2 * hidden]
        activated = gathered[:, 2 * hidden :]
        rows_back = lax.dot_general(
            grad_pre, gate_local, (((1,), (1,)), ((), ())), preferred_element_type=jnp.float32
        ) + lax.dot_general(
            grad_lin, up_local, (((1,), (1,)), ((), ())), preferred_element_type=jnp.float32
        )
        terms = (
            contract_rows(act_rows, grad_pre),
            contract_rows(act_rows, grad_lin),
            contract_rows(activated, cot_rows),
        )
        sums = [t if s is None else s + t for s, t in zip(sums, terms)]
        flat_back = rows_back.astype(jnp.bfloat16).reshape(num_dp * num_exp, take, slice_width)
        arrived = lax.all_to_all(flat_back, axes, split_axis=0, concat_axis=0, tiled=True)
        pieces.append(arrived.reshape(num_dp, num_exp, take, slice_width))
    grad_gate, grad_up, grad_down = (s.astype(jnp.bfloat16)[None] for s in sums)
    arrived = jnp.concatenate(pieces, axis=2).reshape(num_dp, num_exp * capacity, slice_width)
    spread = jnp.broadcast_to(placing[None], (num_dp,) + placing.shape)
    grad_slices = lax.dot_general(
        spread, arrived, (((2,), (1,)), ((0,), (0,))), preferred_element_type=jnp.float32
    ).astype(jnp.bfloat16)
    grad_input = jnp.swapaxes(grad_slices, 0, 1).reshape(tok_rows, width)
    return (grad_input, grad_gate, grad_up, grad_down)


def solution(mesh):
    placed = (
        P(("expert", "dp"), None),
        P(("expert", "dp"), None),
        P(("expert", "dp"), None),
        P(("expert", "dp"), None),
        P("expert", "dp", None),
        P("expert", "dp", None),
        P("expert", None, "dp"),
    )
    return jax.shard_map(
        shards,
        mesh=mesh,
        in_specs=placed,
        out_specs=(
            P(("expert", "dp"), None),
            P("expert", "dp", None),
            P("expert", "dp", None),
            P("expert", None, "dp"),
        ),
        check_vma=False,
    )
```

```python
import jax
import jax.numpy as jnp
from jax import lax
from jax.sharding import PartitionSpec as P


def swiglu_back(gate, upper, upstream):
    sigma = jax.nn.sigmoid(gate)
    silu_gate = gate * sigma
    activated = (silu_gate * upper).astype(jnp.bfloat16)
    grad_pre = (upstream * upper * sigma * (1.0 + gate * (1.0 - sigma))).astype(jnp.bfloat16)
    grad_lin = (upstream * silu_gate).astype(jnp.bfloat16)
    return (grad_pre, grad_lin, activated)


def contract_rows(left, right):
    return lax.dot_general(
        left, right, (((0,), (0,)), ((), ())), preferred_element_type=jnp.float32
    )


def exchange(parts, num_dp):
    rows, cols = parts.shape
    parts = parts.reshape(num_dp, rows // num_dp, cols)
    me = lax.axis_index("dp")
    summed = lax.dynamic_index_in_dim(parts, me, 0, keepdims=False)
    for shift in range(1, num_dp):
        block = lax.dynamic_index_in_dim(parts, (me + shift) % num_dp, 0, keepdims=False)
        pairs = [(i, (i + shift) % num_dp) for i in range(num_dp)]
        came = lax.ppermute(block.astype(jnp.bfloat16), "dp", pairs)
        summed = summed + came.astype(jnp.float32)
    return summed


def shards(
    activations, cotangent, route_ids, route_weights, gate_weights, up_weights, down_weights
):
    tok_rows, width = activations.shape
    topk = route_ids.shape[1]
    num_dp = lax.axis_size("dp")
    num_exp = lax.axis_size("expert")
    slice_width = gate_weights.shape[1]
    hidden = gate_weights.shape[2]
    capacity = min(tok_rows, 5 * tok_rows * topk // (4 * num_exp))
    flat_ids = route_ids.reshape(-1)
    expert_iota = jnp.arange(num_exp, dtype=jnp.int32)
    onehot = (flat_ids[:, None] == expert_iota[None, :]).astype(jnp.int32)
    before = jnp.cumsum(onehot, axis=0) - onehot
    slot = jnp.sum(before * onehot, axis=1)
    target = (flat_ids * capacity + slot).reshape(tok_rows, topk)
    slot_iota = jnp.arange(num_exp * capacity, dtype=jnp.int32)
    matches = target[:, :, None] == slot_iota[None, None, :]
    placing = jnp.any(matches, axis=1).astype(jnp.bfloat16)
    slot_weight = jnp.sum(jnp.where(matches, route_weights[:, :, None], 0.0), axis=(0, 1))
    by_slice = lambda a: jnp.swapaxes(a.reshape(tok_rows, num_dp, slice_width), 0, 1)
    both = jnp.concatenate([by_slice(activations), by_slice(cotangent)], axis=2)
    slots = placing.T.reshape(num_exp, capacity, tok_rows)
    scale = slot_weight.reshape(num_exp, capacity)
    gate_local = gate_weights[0]
    up_local = up_weights[0]
    down_local = down_weights[0]
    axes = ("dp", "expert")
    split = (capacity + 1) // 2
    bounds = [(0, split), (split, capacity)]
    kept = []
    pieces = []
    for lo, hi in bounds:
        take = hi - lo
        rows = num_exp * take
        pick = jnp.broadcast_to(slots[:, lo:hi].reshape(1, rows, tok_rows), (num_dp, rows, tok_rows))
        gathered_rows = lax.dot_general(
            pick, both, (((2,), (1,)), ((0,), (0,))), preferred_element_type=jnp.float32
        )
        weight = jnp.concatenate(
            [
                jnp.ones((rows, slice_width), jnp.float32),
                jnp.broadcast_to(scale[:, lo:hi].reshape(rows, 1), (rows, slice_width)),
            ],
            axis=1,
        )
        flat_both = (gathered_rows * weight[None]).astype(jnp.bfloat16)
        flat_both = flat_both.reshape(num_dp * num_exp, take, 2 * slice_width)
        recv_both = lax.all_to_all(flat_both, axes, split_axis=0, concat_axis=0, tiled=True)
        recv_both = recv_both.reshape(num_exp * num_dp * take, 2 * slice_width)
        act_rows = recv_both[:, :slice_width]
        cot_rows = recv_both[:, slice_width:]
        gate_part = jnp.dot(act_rows, gate_local, preferred_element_type=jnp.float32)
        up_part = jnp.dot(act_rows, up_local, preferred_element_type=jnp.float32)
        back_part = lax.dot_general(
            cot_rows, down_local, (((1,), (1,)), ((), ())), preferred_element_type=jnp.float32
        )
        summed = exchange(jnp.concatenate([gate_part, up_part, back_part], axis=1), num_dp)
        grad_pre, grad_lin, activated = swiglu_back(
            summed[:, :hidden], summed[:, hidden : 2 * hidden], summed[:, 2 * hidden :]
        )
        gathered = lax.all_gather(
            jnp.concatenate([grad_pre, grad_lin, activated], axis=1), "dp", axis=0, tiled=True
        )
        grad_pre = gathered[:, :hidden]
        grad_lin = gathered[:, hidden : 2 * hidden]
        activated = gathered[:, 2 * hidden :]
        rows_back = lax.dot_general(
            grad_pre, gate_local, (((1,), (1,)), ((), ())), preferred_element_type=jnp.float32
        ) + lax.dot_general(
            grad_lin, up_local, (((1,), (1,)), ((), ())), preferred_element_type=jnp.float32
        )
        kept.append((act_rows, cot_rows, grad_pre, grad_lin, activated))
        flat_back = rows_back.astype(jnp.bfloat16).reshape(num_dp * num_exp, take, slice_width)
        arrived = lax.all_to_all(flat_back, axes, split_axis=0, concat_axis=0, tiled=True)
        pieces.append(arrived.reshape(num_dp, num_exp, take, slice_width))
    act_all, cot_all, pre_all, lin_all, activated_all = (
        jnp.concatenate(group, axis=0) for group in zip(*kept)
    )
    grad_gate = contract_rows(act_all, pre_all).astype(jnp.bfloat16)[None]
    grad_up = contract_rows(act_all, lin_all).astype(jnp.bfloat16)[None]
    grad_down = contract_rows(activated_all, cot_all).astype(jnp.bfloat16)[None]
    arrived = jnp.concatenate(pieces, axis=2).reshape(num_dp, num_exp * capacity, slice_width)
    spread = jnp.broadcast_to(placing[None], (num_dp,) + placing.shape)
    grad_slices = lax.dot_general(
        spread, arrived, (((2,), (1,)), ((0,), (0,))), preferred_element_type=jnp.float32
    ).astype(jnp.bfloat16)
    grad_input = jnp.swapaxes(grad_slices, 0, 1).reshape(tok_rows, width)
    return (grad_input, grad_gate, grad_up, grad_down)


def solution(mesh):
    placed = (
        P(("expert", "dp"), None),
        P(("expert", "dp"), None),
        P(("expert", "dp"), None),
        P(("expert", "dp"), None),
        P("expert", "dp", None),
        P("expert", "dp", None),
        P("expert", None, "dp"),
    )
    return jax.shard_map(
        shards,
        mesh=mesh,
        in_specs=placed,
        out_specs=(
            P(("expert", "dp"), None),
            P("expert", "dp", None),
            P("expert", "dp", None),
            P("expert", None, "dp"),
        ),
        check_vma=False,
    )
```

```python
import jax
import jax.numpy as jnp
from jax import lax
from jax.sharding import PartitionSpec as P


def swiglu_back(gate, upper, upstream):
    sigma = jax.nn.sigmoid(gate)
    silu_gate = gate * sigma
    activated = (silu_gate * upper).astype(jnp.bfloat16)
    grad_pre = (upstream * upper * sigma * (1.0 + gate * (1.0 - sigma))).astype(jnp.bfloat16)
    grad_lin = (upstream * silu_gate).astype(jnp.bfloat16)
    return (grad_pre, grad_lin, activated)


def contract_rows(left, right):
    return lax.dot_general(
        left, right, (((0,), (0,)), ((), ())), preferred_element_type=jnp.float32
    )


def exchange(parts, num_dp):
    rows, cols = parts.shape
    parts = parts.reshape(num_dp, rows // num_dp, cols)
    me = lax.axis_index("dp")
    summed = lax.dynamic_index_in_dim(parts, me, 0, keepdims=False)
    for shift in range(1, num_dp):
        block = lax.dynamic_index_in_dim(parts, (me + shift) % num_dp, 0, keepdims=False)
        pairs = [(i, (i + shift) % num_dp) for i in range(num_dp)]
        came = lax.ppermute(block.astype(jnp.bfloat16), "dp", pairs)
        summed = summed + came.astype(jnp.float32)
    return summed


def shards(
    activations, cotangent, route_ids, route_weights, gate_weights, up_weights, down_weights
):
    tok_rows, width = activations.shape
    topk = route_ids.shape[1]
    num_dp = lax.axis_size("dp")
    num_exp = lax.axis_size("expert")
    slice_width = gate_weights.shape[1]
    hidden = gate_weights.shape[2]
    capacity = min(tok_rows, 5 * tok_rows * topk // (4 * num_exp))
    flat_ids = route_ids.reshape(-1)
    expert_iota = jnp.arange(num_exp, dtype=jnp.int32)
    onehot = (flat_ids[:, None] == expert_iota[None, :]).astype(jnp.int32)
    before = jnp.cumsum(onehot, axis=0) - onehot
    slot = jnp.sum(before * onehot, axis=1)
    target = (flat_ids * capacity + slot).reshape(tok_rows, topk)
    slot_iota = jnp.arange(num_exp * capacity, dtype=jnp.int32)
    matches = target[:, :, None] == slot_iota[None, None, :]
    placing = jnp.any(matches, axis=1).astype(jnp.bfloat16)
    slot_weight = jnp.sum(jnp.where(matches, route_weights[:, :, None], 0.0), axis=(0, 1))
    by_slice = lambda a: jnp.swapaxes(a.reshape(tok_rows, num_dp, slice_width), 0, 1)
    both = jnp.concatenate([by_slice(activations), by_slice(cotangent)], axis=2)
    slots = placing.T.reshape(num_exp, capacity, tok_rows)
    scale = slot_weight.reshape(num_exp, capacity)
    gate_local = gate_weights[0]
    up_local = up_weights[0]
    down_local = down_weights[0]
    axes = ("dp", "expert")
    split = (capacity + 1) // 2
    bounds = [(0, split), (split, capacity)]
    kept = []
    pieces = []
    order = jnp.concatenate(
        [slots[:, lo:hi].reshape(num_exp * (hi - lo), tok_rows) for lo, hi in bounds], axis=0
    )
    order_scale = jnp.concatenate(
        [scale[:, lo:hi].reshape(num_exp * (hi - lo), 1) for lo, hi in bounds], axis=0
    )
    all_slots = num_exp * capacity
    pick = jnp.broadcast_to(order[None], (num_dp, all_slots, tok_rows))
    gathered_rows = lax.dot_general(
        pick, both, (((2,), (1,)), ((0,), (0,))), preferred_element_type=jnp.float32
    )
    weight = jnp.concatenate(
        [
            jnp.ones((all_slots, slice_width), jnp.float32),
            jnp.broadcast_to(order_scale, (all_slots, slice_width)),
        ],
        axis=1,
    )
    send_all = (gathered_rows * weight[None]).astype(jnp.bfloat16)
    for lo, hi in bounds:
        take = hi - lo
        start = num_exp * lo
        flat_both = send_all[:, start : start + num_exp * take]
        flat_both = flat_both.reshape(num_dp * num_exp, take, 2 * slice_width)
        recv_both = lax.all_to_all(flat_both, axes, split_axis=0, concat_axis=0, tiled=True)
        recv_both = recv_both.reshape(num_exp * num_dp * take, 2 * slice_width)
        act_rows = recv_both[:, :slice_width]
        cot_rows = recv_both[:, slice_width:]
        gate_part = jnp.dot(act_rows, gate_local, preferred_element_type=jnp.float32)
        up_part = jnp.dot(act_rows, up_local, preferred_element_type=jnp.float32)
        back_part = lax.dot_general(
            cot_rows, down_local, (((1,), (1,)), ((), ())), preferred_element_type=jnp.float32
        )
        summed = exchange(jnp.concatenate([gate_part, up_part, back_part], axis=1), num_dp)
        grad_pre, grad_lin, activated = swiglu_back(
            summed[:, :hidden], summed[:, hidden : 2 * hidden], summed[:, 2 * hidden :]
        )
        gathered = lax.all_gather(
            jnp.concatenate([grad_pre, grad_lin, activated], axis=1), "dp", axis=0, tiled=True
        )
        grad_pre = gathered[:, :hidden]
        grad_lin = gathered[:, hidden : 2 * hidden]
        activated = gathered[:, 2 * hidden :]
        rows_back = lax.dot_general(
            grad_pre, gate_local, (((1,), (1,)), ((), ())), preferred_element_type=jnp.float32
        ) + lax.dot_general(
            grad_lin, up_local, (((1,), (1,)), ((), ())), preferred_element_type=jnp.float32
        )
        kept.append((act_rows, cot_rows, grad_pre, grad_lin, activated))
        flat_back = rows_back.astype(jnp.bfloat16).reshape(num_dp * num_exp, take, slice_width)
        arrived = lax.all_to_all(flat_back, axes, split_axis=0, concat_axis=0, tiled=True)
        pieces.append(arrived.reshape(num_dp, num_exp, take, slice_width))
    act_all, cot_all, pre_all, lin_all, activated_all = (
        jnp.concatenate(group, axis=0) for group in zip(*kept)
    )
    grad_gate = contract_rows(act_all, pre_all).astype(jnp.bfloat16)[None]
    grad_up = contract_rows(act_all, lin_all).astype(jnp.bfloat16)[None]
    grad_down = contract_rows(activated_all, cot_all).astype(jnp.bfloat16)[None]
    arrived = jnp.concatenate(pieces, axis=2).reshape(num_dp, num_exp * capacity, slice_width)
    spread = jnp.broadcast_to(placing[None], (num_dp,) + placing.shape)
    grad_slices = lax.dot_general(
        spread, arrived, (((2,), (1,)), ((0,), (0,))), preferred_element_type=jnp.float32
    ).astype(jnp.bfloat16)
    grad_input = jnp.swapaxes(grad_slices, 0, 1).reshape(tok_rows, width)
    return (grad_input, grad_gate, grad_up, grad_down)


def solution(mesh):
    placed = (
        P(("expert", "dp"), None),
        P(("expert", "dp"), None),
        P(("expert", "dp"), None),
        P(("expert", "dp"), None),
        P("expert", "dp", None),
        P("expert", "dp", None),
        P("expert", None, "dp"),
    )
    return jax.shard_map(
        shards,
        mesh=mesh,
        in_specs=placed,
        out_specs=(
            P(("expert", "dp"), None),
            P("expert", "dp", None),
            P("expert", "dp", None),
            P("expert", None, "dp"),
        ),
        check_vma=False,
    )
```
